256 devices in a mesh: blk: 32 (over x, y, core), req: 8 (over z).
Axes of the slice: x: 4, y: 4, z: 8, core: 2. Of those that a mesh axis runs over, the one named last changes fastest.
Arguments:
- patches: bfloat16 [6144, 1408], P('req')
- vis_ln_gain: bfloat16 [1408], replicated, may hold values from 0.25 to 4
- vis_ln_bias: bfloat16 [1408], replicated, may hold values from -3 to 3
- vis_up: bfloat16 [1408, 6144], P(None, 'blk'), may hold values from -0.15625 to 0.15625
- vis_up_bias: bfloat16 [6144], P('blk'), may hold values from -3 to 3
- vis_down: bfloat16 [6144, 1408], P('blk'), may hold values from -0.15625 to 0.15625
- vis_down_bias: bfloat16 [1408], replicated, may hold values from -3 to 3
- merge_gain: bfloat16 [1408], replicated, may hold values from 0.099609375 to 1.8984375
- merge_proj: bfloat16 [5632, 4096], P(None, 'blk'), may hold values from -0.078125 to 0.078125
- merge_proj_bias: bfloat16 [4096], P('blk'), may hold values from -3 to 3
- image_dest: int32 [1536], replicated, may hold values from 0 to 8191, as said below
- text_embed: bfloat16 [8192, 4096], P('req', 'blk')
- segment_ids: int32 [8, 1024], P('req'), may hold values from 0 to 3, never falling along the last dimension, each value on 1 to 512 neighbouring positions
- text_gain: bfloat16 [4096], replicated, may hold values from 0.099609375 to 1.8984375
- query_weight: bfloat16 [4096, 4096], P(None, 'blk')
- key_weight: bfloat16 [4096, 4096], P(None, 'blk')
- value_weight: bfloat16 [4096, 4096], P(None, 'blk'), may hold values from -0.09375 to 0.09375
- out_weight: bfloat16 [4096, 4096], P('blk'), may hold values from -0.1875 to 0.1875
Outputs:
- hidden_out: bfloat16 [8192, 4096], P(('req', 'blk'))
The draws below stay inside these ranges and needn't reach their ends.
Inputs may be any that keep to these rules, and one draw needn't show every extreme that they name: image_dest holds distinct positions; each group of 1024 positions receives exactly 192 image rows, and of one group's 192 image rows at most 66 go to one group of positions, exactly 66 for one group. `segment_ids`: each row has 4 requests as runs of equal, non-decreasing ids, each of 1 to 512 tokens, one exactly 512.
All inputs are finite; a program needn't handle non-finite values.
Results may differ from the reference program's by a relative error of at most 0.04.
Values may be sent and summed in bfloat16 or wider, within the bound.
No kernel may reach another device: no remote copies, remote signals or barrier semaphores. Data moves between devices by JAX's collectives and lax.ppermute only.
A program may use at most 128 MiB of HBM per device.

```python
import math
import jax
import jax.numpy as jnp
import numpy as np
from jax import lax

VD = 1408
VFF = 6144
D = 4096
HEAD = 128
REQS = 4
PATCH_GRP = 768
TOK_GRP = 1024
MD = 5632
IMG_GRP = 192
SEG_MOST = 512
N_BLK = 32
N_REQ = 8


def scaled_field(key, row_count, col_count):
    key_base, key_rows, key_cols = jax.random.split(key, 3)
    base_values = jax.random.normal(key_base, (row_count, col_count), jnp.float32)
    row_scale = jnp.exp(jax.random.uniform(key_rows, (row_count, 1), jnp.float32, math.log(0.3), math.log(3.0)))
    col_scale = jnp.exp(jax.random.uniform(key_cols, (1, col_count), jnp.float32, math.log(0.3), math.log(3.0)))
    return (base_values * row_scale * col_scale).astype(jnp.bfloat16)


def draw_patches(key, part):
    return scaled_field(key, PATCH_GRP * N_REQ, VD)


def draw_text_embed(key, part):
    return scaled_field(key, TOK_GRP * N_REQ, D)


def draw_query_weight(key, part):
    key_base = jax.random.fold_in(key, 0)
    base_values = jax.random.normal(key_base, (D, D), jnp.float32) * D ** (-0.5)
    return base_values.astype(jnp.bfloat16)


def draw_key_weight(key, part):
    base_values = jax.random.normal(jax.random.fold_in(key, 7), (D, D), jnp.float32) * D ** (-0.5)
    return base_values.astype(jnp.bfloat16)


def draw_image_dest(key, part):
    key_pair, key_order, key_place = jax.random.split(key, 3)
    big_share = IMG_GRP // 4
    other_share = 3 * IMG_GRP // 4 // N_REQ
    partner = jax.random.permutation(key_pair, N_REQ).astype(jnp.int32)
    column_ids = jnp.arange(IMG_GRP, dtype=jnp.int32)[None, :]
    sorted_groups = jnp.where(column_ids < big_share, partner[:, None], (column_ids - big_share) // other_share)
    orders = jax.vmap(lambda each_key: jax.random.permutation(each_key, IMG_GRP))(jax.random.split(key_order, N_REQ))
    groups = jnp.take_along_axis(sorted_groups, orders.astype(jnp.int32), axis=1).reshape(-1).astype(jnp.int32)
    one_hot = (groups[:, None] == jnp.arange(N_REQ, dtype=jnp.int32)[None, :]).astype(jnp.int32)
    arrival = jnp.sum((jnp.cumsum(one_hot, axis=0) - one_hot) * one_hot, axis=1)
    places = jax.vmap(lambda each_key: jax.random.permutation(each_key, TOK_GRP))(jax.random.split(key_place, N_REQ)).astype(jnp.int32)
    return (groups * TOK_GRP + places[groups, arrival]).astype(jnp.int32)


def spiked(values, rng, source, target, shards_of, factor):
    def block_of(dim):
        return (jnp.arange(values.shape[dim]) // (values.shape[dim] // shards_of)).reshape((-1,) + (1,) * (values.ndim - 1 - dim))

    near = jax.random.permutation(rng, shards_of)[block_of(target)]
    far = (block_of(target) + shards_of // 2) % shards_of
    return jnp.where((block_of(source) == near) | (block_of(source) == far), factor * values, values)


def block_levels(stream_key, extent, cuts, low, largest):
    level = 1.0
    for position, parts in cuts:
        draws = jax.random.uniform(jax.random.fold_in(jax.random.fold_in(stream_key, 6), position), (parts,), jnp.float32, low / len(cuts), largest / len(cuts))
        level = level * jnp.repeat(jnp.exp(draws), extent[position] // parts).reshape((-1,) + (1,) * (len(extent) - 1 - position))
    return level


def profile(amount, total, limit, lean):
    weights = [(1 << 20) // math.isqrt(grade ** lean) + 1 for grade in range(2, amount + 1)]
    surplus, holding = total - limit - (amount - 1), [1] * (amount - 1)
    while surplus > 0:
        movable = [i for i in range(amount - 1) if holding[i] < limit]
        pool, remaining = sum([weights[i] for i in movable]), surplus
        for i in movable:
            extra = min(limit - holding[i], max(1, remaining * weights[i] // pool), surplus)
            holding[i] = holding[i] + extra
            surplus = surplus - extra
    return np.array([limit] + holding)


def ragged(own_key, amount, total, reach, slope):
    if amount == 2:
        one = jax.random.randint(own_key, (), max(1, total - reach), min(reach, total - 1) + 1)
        return jnp.stack([one, total - one])
    tallies = jnp.asarray(profile(amount, total, reach, slope), jnp.int32)
    pairs = (amount - 1) // 2
    giver, taker = tallies[1:1 + 2 * pairs:2], tallies[2:2 + 2 * pairs:2]
    margin = jnp.minimum(giver - 1, reach - taker)
    moved = jax.random.randint(jax.random.fold_in(own_key, 1), (pairs,), 0, 1 << 20) % (margin + 1)
    tallies = tallies.at[1:1 + 2 * pairs:2].set(giver - moved).at[2:2 + 2 * pairs:2].set(taker + moved)
    return tallies[jax.random.permutation(jax.random.fold_in(own_key, 2), amount)]


def gaussian(stream_key, extent, scale, limit, shards=(), kind=jnp.bfloat16):
    loudness = block_levels(stream_key, extent, shards, -0.22, 0.18) if shards else 1.0
    values = jax.random.normal(stream_key, extent, jnp.float32) * scale * loudness
    return jnp.minimum(jnp.maximum(values, -limit), limit).astype(kind)


def noise_with(rng, shape, deviation, most, cuts, heavy, kind=jnp.bfloat16):
    entries = deviation * jax.random.normal(rng, shape, jnp.float32)
    if cuts:
        entries = entries * block_levels(rng, shape, cuts, -0.22, 0.18)
    return jnp.clip(spiked(entries, jax.random.fold_in(rng, 3), *heavy), -most, most).astype(kind)


def setup_inputs(seed: int = 0) -> dict:
    streams_of = jax.random.split(jax.random.key(seed), 19)
    patches = draw_patches(jax.random.fold_in(streams_of[18], 71), 0)
    vis_ln_gain = jnp.clip(jnp.exp(jax.random.uniform(streams_of[1], (VD,), jnp.float32, math.log(0.25), math.log(4.0))), 0.25, 4.0).astype(jnp.bfloat16)
    vis_ln_bias = gaussian(streams_of[2], (VD,), 0.5, 3.0)
    vis_up = gaussian(streams_of[3], (VD, VFF), VD ** -0.5, 0.15625, ((1, 32),))
    vis_up_bias = gaussian(streams_of[4], (VFF,), 0.5, 3.0, ((0, 32),))
    vis_down = noise_with(streams_of[5], (VFF, VD), VFF ** -0.5, 0.15625, ((0, 32),), (0, 1, 32, 2.75))
    vis_down_bias = gaussian(streams_of[6], (VD,), 0.5, 3.0)
    merge_gain = jnp.clip(1.0 + 0.18 * jax.random.normal(streams_of[7], (VD,), jnp.float32), 0.099609375, 1.8984375).astype(jnp.bfloat16)
    merge_proj = gaussian(streams_of[8], (MD, D), MD ** -0.5, 0.078125, ((1, 32),))
    merge_proj_bias = gaussian(streams_of[9], (D,), 0.5, 3.0, ((0, 32),))
    image_dest = draw_image_dest(jax.random.fold_in(streams_of[18], 71), 0)
    text_embed = draw_text_embed(jax.random.fold_in(streams_of[18], 71), 0)
    segment_ids = jax.vmap(lambda own: jnp.searchsorted(jnp.cumsum(ragged(own, REQS, TOK_GRP, SEG_MOST, 2)), jnp.arange(TOK_GRP), side="right"))(jax.random.split(streams_of[12], N_REQ)).reshape((N_REQ, TOK_GRP)).astype(jnp.int32)
    text_gain = jnp.clip(1.0 + 0.18 * jax.random.normal(streams_of[13], (D,), jnp.float32), 0.099609375, 1.8984375).astype(jnp.bfloat16)
    query_weight = draw_query_weight(jax.random.fold_in(streams_of[18], 71), 0)
    key_weight = draw_key_weight(jax.random.fold_in(streams_of[18], 71), 0)
    value_weight = gaussian(streams_of[16], (D, D), D ** -0.5, 0.09375, ((1, 32),))
    out_weight = noise_with(streams_of[17], (D, D), D ** -0.5, 0.1875, ((0, 32),), (0, 1, 32, 2.75))
    return dict(patches=patches, vis_ln_gain=vis_ln_gain, vis_ln_bias=vis_ln_bias, vis_up=vis_up, vis_up_bias=vis_up_bias, vis_down=vis_down, vis_down_bias=vis_down_bias, merge_gain=merge_gain, merge_proj=merge_proj, merge_proj_bias=merge_proj_bias, image_dest=image_dest, text_embed=text_embed, segment_ids=segment_ids, text_gain=text_gain, query_weight=query_weight, key_weight=key_weight, value_weight=value_weight, out_weight=out_weight)


def layer_norm(values, gain_vector, shift_vector):
    centre = lax.optimization_barrier(jnp.mean(values, axis=-1, keepdims=True))
    centred = values - centre
    spread = lax.optimization_barrier(jnp.mean(centred * centred, axis=-1, keepdims=True))
    result = centred * lax.rsqrt(spread + 1e-06) * gain_vector.astype(jnp.float32)
    if shift_vector is None:
        return result
    return result + shift_vector.astype(jnp.float32)

def rotate(values, positions):
    half_size = HEAD // 2
    frequency = 10000.0 ** (-2.0 * jnp.arange(half_size, dtype=jnp.float32) / HEAD)
    angles = positions.astype(jnp.float32)[:, None] * frequency[None, :]
    cosine = jnp.cos(angles)[:, None, :]
    sine_table = jnp.sin(angles)[:, None, :]
    by_head = values.reshape(values.shape[0], -1, HEAD)
    first_half = by_head[..., :half_size]
    second_half = by_head[..., half_size:]
    turned = jnp.concatenate([first_half * cosine - second_half * sine_table, second_half * cosine + first_half * sine_table], axis=-1)
    return turned.reshape(values.shape)

def causal_setup(segments):
    length = segments.shape[0]
    column_ids = jnp.arange(length)
    same_request = segments[:, None] == segments[None, :]
    earlier = column_ids[None, :] < column_ids[:, None]
    positions = lax.optimization_barrier(jnp.sum(same_request & earlier, axis=1)).astype(jnp.int32)
    allowed = same_request & (column_ids[None, :] <= column_ids[:, None])
    return (positions, allowed)

def attend(queries, keys, values, allowed):
    length = queries.shape[0]
    query_heads = queries.reshape(length, -1, HEAD).astype(jnp.float32)
    key_heads = keys.reshape(length, -1, HEAD).astype(jnp.float32)
    value_heads = values.reshape(length, -1, HEAD).astype(jnp.float32)
    scores = jnp.einsum('thd,shd->hts', query_heads, key_heads) * HEAD ** (-0.5)
    scores = jnp.where(allowed[None, :, :], scores, -jnp.inf)
    top_score = lax.optimization_barrier(jnp.max(scores, axis=-1, keepdims=True))
    weights = jnp.exp(scores - top_score)
    weights = (weights / lax.optimization_barrier(jnp.sum(weights, axis=-1, keepdims=True))).astype(jnp.bfloat16)
    mixed = jnp.einsum('hts,shd->thd', weights.astype(jnp.float32), value_heads)
    return mixed.astype(jnp.bfloat16).reshape(length, -1)

def blocked_sum(left, right, blocks):
    total_rows, inner_size = left.shape
    block_width = inner_size // blocks
    left_blocks = left.reshape(total_rows, blocks, block_width).transpose(1, 0, 2)
    right_blocks = right.reshape(blocks, block_width, right.shape[1])

    def add_block(running, block_pair):
        product = jnp.dot(block_pair[0], block_pair[1], preferred_element_type=jnp.float32).astype(jnp.bfloat16)
        product = lax.optimization_barrier(product)
        return (running + product.astype(jnp.float32), None)
    initial = jnp.zeros((total_rows, right.shape[1]), jnp.float32)
    summed, unused = lax.scan(add_block, initial, (left_blocks, right_blocks))
    return summed

def reference(patches, vis_ln_gain, vis_ln_bias, vis_up, vis_up_bias, vis_down, vis_down_bias, merge_gain, merge_proj, merge_proj_bias, image_dest, text_embed, segment_ids, text_gain, query_weight, key_weight, value_weight, out_weight):
    patch_values = patches.astype(jnp.float32)
    normed = layer_norm(patch_values, vis_ln_gain, vis_ln_bias).astype(jnp.bfloat16)
    pre_act = jnp.dot(normed, vis_up, preferred_element_type=jnp.float32) + vis_up_bias.astype(jnp.float32)
    hidden = jax.nn.gelu(pre_act, approximate=False).astype(jnp.bfloat16)
    vis_mlp = blocked_sum(hidden, vis_down, N_BLK)
    vis_out = patch_values + vis_mlp + vis_down_bias.astype(jnp.float32)
    merge_in = layer_norm(vis_out, merge_gain, None).astype(jnp.bfloat16).reshape(-1, 4 * VD)
    image = (jnp.dot(merge_in, merge_proj, preferred_element_type=jnp.float32) + merge_proj_bias.astype(jnp.float32)).astype(jnp.bfloat16)
    tokens = text_embed.at[image_dest].set(image)
    grouped = tokens.reshape(N_REQ, TOK_GRP, D)

    def one_group(group_pair):
        token_values = group_pair[0].astype(jnp.float32)
        normed_tokens = (token_values * lax.rsqrt(lax.optimization_barrier(jnp.mean(token_values * token_values, axis=-1, keepdims=True)) + 1e-05) * text_gain.astype(jnp.float32)).astype(jnp.bfloat16)
        positions, allowed = causal_setup(group_pair[1])
        queries = rotate(jnp.dot(normed_tokens, query_weight, preferred_element_type=jnp.float32), positions).astype(jnp.bfloat16)
        keys_rot = rotate(jnp.dot(normed_tokens, key_weight, preferred_element_type=jnp.float32), positions).astype(jnp.bfloat16)
        values_all = jnp.dot(normed_tokens, value_weight, preferred_element_type=jnp.float32).astype(jnp.bfloat16)
        attn = attend(queries, keys_rot, values_all, allowed)
        attn_sum = blocked_sum(attn, out_weight, N_BLK)
        return (token_values + attn_sum).astype(jnp.bfloat16)
    return lax.map(one_group, (grouped, segment_ids)).reshape(N_REQ * TOK_GRP, D)
```

```python
import jax
import jax.numpy as jnp
from jax import lax
from jax.sharding import PartitionSpec as P

HEAD = 128


def layer_norm(values, gain_vector, shift_vector):
    centre = jnp.mean(values, axis=-1, keepdims=True)
    centred = values - centre
    spread = jnp.mean(centred * centred, axis=-1, keepdims=True)
    result = centred * lax.rsqrt(spread + 1e-06) * gain_vector.astype(jnp.float32)
    if shift_vector is None:
        return result
    return result + shift_vector.astype(jnp.float32)


def rotate(values, positions):
    half_size = HEAD // 2
    frequency = 10000.0 ** (-2.0 * jnp.arange(half_size, dtype=jnp.float32) / HEAD)
    angles = positions.astype(jnp.float32)[:, None] * frequency[None, :]
    cosine = jnp.cos(angles)[:, None, :]
    sine_table = jnp.sin(angles)[:, None, :]
    by_head = values.reshape(values.shape[0], -1, HEAD)
    first_half = by_head[..., :half_size]
    second_half = by_head[..., half_size:]
    turned = jnp.concatenate(
        [
            first_half * cosine - second_half * sine_table,
            second_half * cosine + first_half * sine_table,
        ],
        axis=-1,
    )
    return turned.reshape(values.shape)


def causal_setup(segments):
    length = segments.shape[0]
    column_ids = jnp.arange(length)
    same_request = segments[:, None] == segments[None, :]
    earlier = column_ids[None, :] < column_ids[:, None]
    positions = jnp.sum(same_request & earlier, axis=1)
    allowed = same_request & (column_ids[None, :] <= column_ids[:, None])
    return (positions, allowed)


def attend(queries, keys, values, allowed):
    row_count = queries.shape[0]
    key_count = keys.shape[0]
    query_heads = queries.reshape(row_count, -1, HEAD)
    key_heads = keys.reshape(key_count, -1, HEAD)
    value_heads = values.reshape(key_count, -1, HEAD)
    scores = jnp.einsum(
        "thd,shd->hts", query_heads, key_heads, preferred_element_type=jnp.float32
    ) * HEAD ** (-0.5)
    scores = jnp.where(allowed[None, :, :], scores, -jnp.inf)
    top_score = jnp.max(scores, axis=-1, keepdims=True)
    weights = jnp.exp(scores - top_score)
    weights = (weights / jnp.sum(weights, axis=-1, keepdims=True)).astype(jnp.bfloat16)
    mixed = jnp.einsum("hts,shd->thd", weights, value_heads, preferred_element_type=jnp.float32)
    return mixed.astype(jnp.bfloat16).reshape(row_count, -1)


def body(
    patches,
    vis_ln_gain,
    vis_ln_bias,
    vis_up,
    vis_up_bias,
    vis_down,
    vis_down_bias,
    merge_gain,
    merge_proj,
    merge_proj_bias,
    image_dest,
    text_embed,
    segment_ids,
    text_gain,
    query_weight,
    key_weight,
    value_weight,
    out_weight,
):
    blk_count = lax.axis_size("blk")
    req_count = lax.axis_size("req")
    blk_index = lax.axis_index("blk")
    req_index = lax.axis_index("req")
    vis_width = patches.shape[1]
    patch_rows = patches.astype(jnp.float32)
    normed = layer_norm(patch_rows, vis_ln_gain, vis_ln_bias).astype(jnp.bfloat16)
    pre_act = jnp.dot(normed, vis_up, preferred_element_type=jnp.float32) + vis_up_bias.astype(
        jnp.float32
    )
    hidden = jax.nn.gelu(pre_act, approximate=False).astype(jnp.bfloat16)
    partial = jnp.dot(hidden, vis_down, preferred_element_type=jnp.float32).astype(jnp.bfloat16)
    patch_count = patches.shape[0]
    row_share = patch_count // blk_count
    parts_here = lax.all_to_all(
        partial.reshape(blk_count, row_share, vis_width), "blk", 0, 0, tiled=False
    )
    summed = jnp.sum(parts_here.astype(jnp.float32), axis=0)
    own_rows = lax.dynamic_slice_in_dim(patch_rows, blk_index * row_share, row_share, 0)
    vis_out = own_rows + summed + vis_down_bias.astype(jnp.float32)
    normed = layer_norm(vis_out, merge_gain, None).astype(jnp.bfloat16)
    merged_here = normed.reshape(-1, 4 * vis_width)
    merged_all = lax.all_to_all(
        jnp.broadcast_to(merged_here[None], (blk_count,) + merged_here.shape),
        "blk",
        0,
        0,
        tiled=False,
    )
    image_cols = jnp.dot(
        merged_all.reshape(-1, 4 * vis_width), merge_proj, preferred_element_type=jnp.float32
    )
    image_cols = (image_cols + merge_proj_bias.astype(jnp.float32)).astype(jnp.bfloat16)
    image_count = image_cols.shape[0]
    col_width = image_cols.shape[1]
    tok_grp = text_embed.shape[0]
    dest_group = image_dest // tok_grp
    dest_local = image_dest - dest_group * tok_grp
    target = jnp.where(dest_group == req_index, dest_local, tok_grp)
    filler = jnp.zeros((1, col_width), jnp.bfloat16)
    capacity = image_count // 4 + 3 * image_count // 4 // req_count
    by_source = dest_group.reshape(req_count, image_count)
    one_hot = (
        by_source[:, :, None] == jnp.arange(req_count, dtype=jnp.int32)[None, None, :]
    ).astype(jnp.int32)
    slot_index = jnp.sum((jnp.cumsum(one_hot, axis=1) - one_hot) * one_hot, axis=2)
    send_slot = lax.dynamic_index_in_dim(
        by_source * capacity + slot_index, req_index, 0, keepdims=False
    )
    source_row = (
        jnp.full((req_count * capacity,), image_count, jnp.int32)
        .at[send_slot]
        .set(jnp.arange(image_count, dtype=jnp.int32))
    )
    outgoing = jnp.take(jnp.concatenate([image_cols, filler], axis=0), source_row, axis=0)
    incoming = lax.all_to_all(outgoing, "req", split_axis=0, concat_axis=0, tiled=True)
    arrival = (jnp.arange(req_count, dtype=jnp.int32)[:, None] * capacity + slot_index).reshape(-1)
    row_table = jnp.concatenate([incoming, filler], axis=0)
    missing = row_table.shape[0] - 1
    lookup = jnp.full((tok_grp,), missing, jnp.int32).at[target].set(arrival, mode="drop")
    columns = jnp.where(
        (lookup < missing)[:, None], jnp.take(row_table, lookup, axis=0), text_embed
    )
    features = lax.all_gather(columns, "blk", axis=1, tiled=True)
    token_values = features.astype(jnp.float32)
    normed_tokens = (
        token_values
        * lax.rsqrt(jnp.mean(token_values * token_values, axis=-1, keepdims=True) + 1e-05)
        * text_gain.astype(jnp.float32)
    ).astype(jnp.bfloat16)
    positions, allowed = causal_setup(segment_ids[0])
    queries = rotate(
        jnp.dot(normed_tokens, query_weight, preferred_element_type=jnp.float32), positions
    ).astype(jnp.bfloat16)
    keys_rot = rotate(
        jnp.dot(normed_tokens, key_weight, preferred_element_type=jnp.float32), positions
    ).astype(jnp.bfloat16)
    values_here = jnp.dot(normed_tokens, value_weight, preferred_element_type=jnp.float32).astype(
        jnp.bfloat16
    )
    block_rows = min(512, tok_grp)
    block_count = tok_grp // block_rows

    def attend_block(block_pair):
        return attend(block_pair[0], keys_rot, values_here, block_pair[1])

    attn_out = lax.map(
        attend_block,
        (
            queries.reshape(block_count, block_rows, -1),
            allowed.reshape(block_count, block_rows, tok_grp),
        ),
    ).reshape(tok_grp, -1)
    out_share = tok_grp // blk_count
    summed_heads = lax.psum_scatter(
        jnp.dot(attn_out, out_weight, preferred_element_type=jnp.float32).astype(jnp.bfloat16),
        "blk",
        scatter_dimension=0,
        tiled=True,
    ).astype(jnp.float32)
    residual = lax.dynamic_slice_in_dim(token_values, blk_index * out_share, out_share, 0)
    return (residual + summed_heads).astype(jnp.bfloat16)


def solution(mesh):
    return jax.shard_map(
        body,
        mesh=mesh,
        in_specs=(
            P("req", None),
            P(),
            P(),
            P(None, "blk"),
            P("blk"),
            P("blk", None),
            P(),
            P(),
            P(None, "blk"),
            P("blk"),
            P(),
            P("req", "blk"),
            P("req", None),
            P(),
            P(None, "blk"),
            P(None, "blk"),
            P(None, "blk"),
            P("blk", None),
        ),
        out_specs=P(("req", "blk"), None),
        check_vma=False,
    )
```

```python
import jax
import jax.numpy as jnp
from jax import lax
from jax.sharding import PartitionSpec as P

HEAD = 128


def layer_norm(values, gain_vector, shift_vector):
    centre = jnp.mean(values, axis=-1, keepdims=True)
    centred = values - centre
    spread = jnp.mean(centred * centred, axis=-1, keepdims=True)
    result = centred * lax.rsqrt(spread + 1e-06) * gain_vector.astype(jnp.float32)
    if shift_vector is None:
        return result
    return result + shift_vector.astype(jnp.float32)


def rotate(values, positions):
    half_size = HEAD // 2
    frequency = 10000.0 ** (-2.0 * jnp.arange(half_size, dtype=jnp.float32) / HEAD)
    angles = positions.astype(jnp.float32)[:, None] * frequency[None, :]
    cosine = jnp.cos(angles)[:, None, :]
    sine_table = jnp.sin(angles)[:, None, :]
    by_head = values.reshape(values.shape[0], -1, HEAD)
    first_half = by_head[..., :half_size]
    second_half = by_head[..., half_size:]
    turned = jnp.concatenate(
        [
            first_half * cosine - second_half * sine_table,
            second_half * cosine + first_half * sine_table,
        ],
        axis=-1,
    )
    return turned.reshape(values.shape)


def causal_setup(segments):
    length = segments.shape[0]
    column_ids = jnp.arange(length)
    same_request = segments[:, None] == segments[None, :]
    earlier = column_ids[None, :] < column_ids[:, None]
    positions = jnp.sum(same_request & earlier, axis=1)
    allowed = same_request & (column_ids[None, :] <= column_ids[:, None])
    return (positions, allowed)


def attend(queries, keys, values, allowed):
    row_count = queries.shape[0]
    key_count = keys.shape[0]
    query_heads = queries.reshape(row_count, -1, HEAD)
    key_heads = keys.reshape(key_count, -1, HEAD)
    value_heads = values.reshape(key_count, -1, HEAD)
    scores = jnp.einsum(
        "thd,shd->hts", query_heads, key_heads, preferred_element_type=jnp.float32
    ) * HEAD ** (-0.5)
    scores = jnp.where(allowed[None, :, :], scores, -jnp.inf)
    top_score = jnp.max(scores, axis=-1, keepdims=True)
    weights = jnp.exp(scores - top_score)
    weights = (weights / jnp.sum(weights, axis=-1, keepdims=True)).astype(jnp.bfloat16)
    mixed = jnp.einsum("hts,shd->thd", weights, value_heads, preferred_element_type=jnp.float32)
    return mixed.astype(jnp.bfloat16).reshape(row_count, -1)


def body(
    patches,
    vis_ln_gain,
    vis_ln_bias,
    vis_up,
    vis_up_bias,
    vis_down,
    vis_down_bias,
    merge_gain,
    merge_proj,
    merge_proj_bias,
    image_dest,
    text_embed,
    segment_ids,
    text_gain,
    query_weight,
    key_weight,
    value_weight,
    out_weight,
):
    blk_count = lax.axis_size("blk")
    req_count = lax.axis_size("req")
    blk_index = lax.axis_index("blk")
    req_index = lax.axis_index("req")
    vis_width = patches.shape[1]
    patch_rows = patches.astype(jnp.float32)
    normed = layer_norm(patch_rows, vis_ln_gain, vis_ln_bias).astype(jnp.bfloat16)
    pre_act = jnp.dot(normed, vis_up, preferred_element_type=jnp.float32) + vis_up_bias.astype(
        jnp.float32
    )
    hidden = jax.nn.gelu(pre_act, approximate=False).astype(jnp.bfloat16)
    partial = jnp.dot(hidden, vis_down, preferred_element_type=jnp.float32).astype(jnp.bfloat16)
    patch_count = patches.shape[0]
    row_share = patch_count // blk_count
    parts_here = lax.all_to_all(
        partial.reshape(blk_count, row_share, vis_width), "blk", 0, 0, tiled=False
    )
    summed = jnp.sum(parts_here.astype(jnp.float32), axis=0)
    own_rows = lax.dynamic_slice_in_dim(patch_rows, blk_index * row_share, row_share, 0)
    vis_out = own_rows + summed + vis_down_bias.astype(jnp.float32)
    normed = layer_norm(vis_out, merge_gain, None).astype(jnp.bfloat16)
    merged_here = normed.reshape(-1, 4 * vis_width)
    merged_all = lax.all_to_all(
        jnp.broadcast_to(merged_here[None], (blk_count,) + merged_here.shape),
        "blk",
        0,
        0,
        tiled=False,
    )
    image_cols = jnp.dot(
        merged_all.reshape(-1, 4 * vis_width), merge_proj, preferred_element_type=jnp.float32
    )
    image_cols = (image_cols + merge_proj_bias.astype(jnp.float32)).astype(jnp.bfloat16)
    image_count = image_cols.shape[0]
    col_width = image_cols.shape[1]
    tok_grp = text_embed.shape[0]
    dest_group = image_dest // tok_grp
    dest_local = image_dest - dest_group * tok_grp
    target = jnp.where(dest_group == req_index, dest_local, tok_grp)
    filler = jnp.zeros((1, col_width), jnp.bfloat16)
    capacity = image_count // 4 + 3 * image_count // 4 // req_count
    by_source = dest_group.reshape(req_count, image_count)
    one_hot = (
        by_source[:, :, None] == jnp.arange(req_count, dtype=jnp.int32)[None, None, :]
    ).astype(jnp.int32)
    slot_index = jnp.sum((jnp.cumsum(one_hot, axis=1) - one_hot) * one_hot, axis=2)
    send_slot = lax.dynamic_index_in_dim(
        by_source * capacity + slot_index, req_index, 0, keepdims=False
    )
    source_row = (
        jnp.full((req_count * capacity,), image_count, jnp.int32)
        .at[send_slot]
        .set(jnp.arange(image_count, dtype=jnp.int32))
    )
    outgoing = jnp.take(jnp.concatenate([image_cols, filler], axis=0), source_row, axis=0)
    incoming = lax.all_to_all(outgoing, "req", split_axis=0, concat_axis=0, tiled=True)
    arrival = (jnp.arange(req_count, dtype=jnp.int32)[:, None] * capacity + slot_index).reshape(-1)
    row_table = jnp.concatenate([incoming, filler], axis=0)
    missing = row_table.shape[0] - 1
    lookup = jnp.full((tok_grp,), missing, jnp.int32).at[target].set(arrival, mode="drop")
    columns = jnp.where(
        (lookup < missing)[:, None], jnp.take(row_table, lookup, axis=0), text_embed
    )
    features = lax.all_gather(columns, "blk", axis=1, tiled=True)
    token_values = features.astype(jnp.float32)
    normed_tokens = (
        token_values
        * lax.rsqrt(jnp.mean(token_values * token_values, axis=-1, keepdims=True) + 1e-05)
        * text_gain.astype(jnp.float32)
    ).astype(jnp.bfloat16)
    positions, allowed = causal_setup(segment_ids[0])
    queries = rotate(
        jnp.dot(normed_tokens, query_weight, preferred_element_type=jnp.float32), positions
    ).astype(jnp.bfloat16)
    keys_rot = rotate(
        jnp.dot(normed_tokens, key_weight, preferred_element_type=jnp.float32), positions
    ).astype(jnp.bfloat16)
    values_here = jnp.dot(normed_tokens, value_weight, preferred_element_type=jnp.float32).astype(
        jnp.bfloat16
    )
    block_rows = min(512, tok_grp)
    block_count = tok_grp // block_rows

    def attend_block(block_pair):
        return attend(block_pair[0], keys_rot, values_here, block_pair[1])

    attn_out = lax.map(
        attend_block,
        (
            queries.reshape(block_count, block_rows, -1),
            allowed.reshape(block_count, block_rows, tok_grp),
        ),
    ).reshape(tok_grp, -1)
    out_share = tok_grp // blk_count
    head_part = jnp.dot(attn_out, out_weight, preferred_element_type=jnp.float32).astype(
        jnp.bfloat16
    )
    heads_here = lax.all_to_all(
        head_part.reshape(blk_count, out_share, head_part.shape[1]), "blk", 0, 0, tiled=False
    )
    summed_heads = jnp.sum(heads_here.astype(jnp.float32), axis=0)
    residual = lax.dynamic_slice_in_dim(token_values, blk_index * out_share, out_share, 0)
    return (residual + summed_heads).astype(jnp.bfloat16)


def solution(mesh):
    return jax.shard_map(
        body,
        mesh=mesh,
        in_specs=(
            P("req", None),
            P(),
            P(),
            P(None, "blk"),
            P("blk"),
            P("blk", None),
            P(),
            P(),
            P(None, "blk"),
            P("blk"),
            P(),
            P("req", "blk"),
            P("req", None),
            P(),
            P(None, "blk"),
            P(None, "blk"),
            P(None, "blk"),
            P("blk", None),
        ),
        out_specs=P(("req", "blk"), None),
        check_vma=False,
    )
```

```python
import jax
import jax.numpy as jnp
from jax import lax
from jax.sharding import PartitionSpec as P

HEAD = 128


def layer_norm(values, gain_vector, shift_vector):
    centre = jnp.mean(values, axis=-1, keepdims=True)
    centred = values - centre
    spread = jnp.mean(centred * centred, axis=-1, keepdims=True)
    result = centred * lax.rsqrt(spread + 1e-06) * gain_vector.astype(jnp.float32)
    if shift_vector is None:
        return result
    return result + shift_vector.astype(jnp.float32)


def rotate(values, positions):
    half_size = HEAD // 2
    frequency = 10000.0 ** (-2.0 * jnp.arange(half_size, dtype=jnp.float32) / HEAD)
    angles = positions.astype(jnp.float32)[:, None] * frequency[None, :]
    cosine = jnp.cos(angles)[:, None, :]
    sine_table = jnp.sin(angles)[:, None, :]
    by_head = values.reshape(values.shape[0], -1, HEAD)
    first_half = by_head[..., :half_size]
    second_half = by_head[..., half_size:]
    turned = jnp.concatenate(
        [
            first_half * cosine - second_half * sine_table,
            second_half * cosine + first_half * sine_table,
        ],
        axis=-1,
    )
    return turned.reshape(values.shape)


def causal_setup(segments):
    length = segments.shape[0]
    column_ids = jnp.arange(length)
    same_request = segments[:, None] == segments[None, :]
    earlier = column_ids[None, :] < column_ids[:, None]
    positions = jnp.sum(same_request & earlier, axis=1)
    allowed = same_request & (column_ids[None, :] <= column_ids[:, None])
    return (positions, allowed)


def attend(queries, keys, values, allowed):
    row_count = queries.shape[0]
    key_count = keys.shape[0]
    query_heads = queries.reshape(row_count, -1, HEAD)
    key_heads = keys.reshape(key_count, -1, HEAD)
    value_heads = values.reshape(key_count, -1, HEAD)
    scores = jnp.einsum(
        "thd,shd->hts", query_heads, key_heads, preferred_element_type=jnp.float32
    ) * HEAD ** (-0.5)
    scores = jnp.where(allowed[None, :, :], scores, -jnp.inf)
    top_score = jnp.max(scores, axis=-1, keepdims=True)
    weights = jnp.exp(scores - top_score)
    weights = (weights / jnp.sum(weights, axis=-1, keepdims=True)).astype(jnp.bfloat16)
    mixed = jnp.einsum("hts,shd->thd", weights, value_heads, preferred_element_type=jnp.float32)
    return mixed.astype(jnp.bfloat16).reshape(row_count, -1)


def body(
    patches,
    vis_ln_gain,
    vis_ln_bias,
    vis_up,
    vis_up_bias,
    vis_down,
    vis_down_bias,
    merge_gain,
    merge_proj,
    merge_proj_bias,
    image_dest,
    text_embed,
    segment_ids,
    text_gain,
    query_weight,
    key_weight,
    value_weight,
    out_weight,
):
    blk_count = lax.axis_size("blk")
    req_count = lax.axis_size("req")
    blk_index = lax.axis_index("blk")
    req_index = lax.axis_index("req")
    vis_width = patches.shape[1]
    gathered_text = lax.all_gather(text_embed, "blk", axis=1, tiled=True)
    patch_rows = patches.astype(jnp.float32)
    normed = layer_norm(patch_rows, vis_ln_gain, vis_ln_bias).astype(jnp.bfloat16)
    pre_act = jnp.dot(normed, vis_up, preferred_element_type=jnp.float32) + vis_up_bias.astype(
        jnp.float32
    )
    hidden = jax.nn.gelu(pre_act, approximate=False).astype(jnp.bfloat16)
    partial = jnp.dot(hidden, vis_down, preferred_element_type=jnp.float32).astype(jnp.bfloat16)
    patch_count = patches.shape[0]
    row_share = patch_count // blk_count
    parts_here = lax.all_to_all(
        partial.reshape(blk_count, row_share, vis_width), "blk", 0, 0, tiled=False
    )
    summed = jnp.sum(parts_here.astype(jnp.float32), axis=0)
    own_rows = lax.dynamic_slice_in_dim(patch_rows, blk_index * row_share, row_share, 0)
    vis_out = own_rows + summed + vis_down_bias.astype(jnp.float32)
    normed = layer_norm(vis_out, merge_gain, None).astype(jnp.bfloat16)
    merged_here = normed.reshape(-1, 4 * vis_width)
    merged_all = lax.all_to_all(
        jnp.broadcast_to(merged_here[None], (blk_count,) + merged_here.shape),
        "blk",
        0,
        0,
        tiled=False,
    )
    image_cols = jnp.dot(
        merged_all.reshape(-1, 4 * vis_width), merge_proj, preferred_element_type=jnp.float32
    )
    image_cols = (image_cols + merge_proj_bias.astype(jnp.float32)).astype(jnp.bfloat16)
    image_count = image_cols.shape[0]
    col_width = image_cols.shape[1]
    tok_grp = text_embed.shape[0]
    dest_group = image_dest // tok_grp
    dest_local = image_dest - dest_group * tok_grp
    target = jnp.where(dest_group == req_index, dest_local, tok_grp)
    filler = jnp.zeros((1, col_width), jnp.bfloat16)
    capacity = image_count // 4 + 3 * image_count // 4 // req_count
    by_source = dest_group.reshape(req_count, image_count)
    one_hot = (
        by_source[:, :, None] == jnp.arange(req_count, dtype=jnp.int32)[None, None, :]
    ).astype(jnp.int32)
    slot_index = jnp.sum((jnp.cumsum(one_hot, axis=1) - one_hot) * one_hot, axis=2)
    send_slot = lax.dynamic_index_in_dim(
        by_source * capacity + slot_index, req_index, 0, keepdims=False
    )
    source_row = (
        jnp.full((req_count * capacity,), image_count, jnp.int32)
        .at[send_slot]
        .set(jnp.arange(image_count, dtype=jnp.int32))
    )
    outgoing = jnp.take(jnp.concatenate([image_cols, filler], axis=0), source_row, axis=0)
    incoming = lax.all_to_all(outgoing, "req", split_axis=0, concat_axis=0, tiled=True)
    arrival = (jnp.arange(req_count, dtype=jnp.int32)[:, None] * capacity + slot_index).reshape(-1)
    mine = (dest_group == req_index).astype(jnp.int32)
    rank = jnp.cumsum(mine) - mine
    total_images = image_dest.shape[0]
    pick = (
        jnp.zeros((image_count,), jnp.int32)
        .at[jnp.where(mine > 0, rank, image_count)]
        .set(jnp.arange(total_images, dtype=jnp.int32), mode="drop")
    )
    mine_cols = jnp.take(incoming, jnp.take(arrival, pick), axis=0)
    mine_rows = lax.all_to_all(
        jnp.broadcast_to(mine_cols[None], (blk_count,) + mine_cols.shape), "blk", 0, 0, tiled=False
    )
    mine_rows = mine_rows.transpose(1, 0, 2).reshape(image_count, -1)
    lookup = (
        jnp.full((tok_grp,), image_count, jnp.int32)
        .at[jnp.take(dest_local, pick)]
        .set(jnp.arange(image_count, dtype=jnp.int32))
    )
    row_table = jnp.concatenate([mine_rows, jnp.zeros_like(mine_rows[:1])], axis=0)
    features = jnp.where(
        (lookup < image_count)[:, None], jnp.take(row_table, lookup, axis=0), gathered_text
    )
    token_values = features.astype(jnp.float32)
    normed_tokens = (
        token_values
        * lax.rsqrt(jnp.mean(token_values * token_values, axis=-1, keepdims=True) + 1e-05)
        * text_gain.astype(jnp.float32)
    ).astype(jnp.bfloat16)
    positions, allowed = causal_setup(segment_ids[0])
    queries = rotate(
        jnp.dot(normed_tokens, query_weight, preferred_element_type=jnp.float32), positions
    ).astype(jnp.bfloat16)
    keys_rot = rotate(
        jnp.dot(normed_tokens, key_weight, preferred_element_type=jnp.float32), positions
    ).astype(jnp.bfloat16)
    values_here = jnp.dot(normed_tokens, value_weight, preferred_element_type=jnp.float32).astype(
        jnp.bfloat16
    )
    block_rows = min(512, tok_grp)
    block_count = tok_grp // block_rows

    def attend_block(block_pair):
        return attend(block_pair[0], keys_rot, values_here, block_pair[1])

    attn_out = lax.map(
        attend_block,
        (
            queries.reshape(block_count, block_rows, -1),
            allowed.reshape(block_count, block_rows, tok_grp),
        ),
    ).reshape(tok_grp, -1)
    out_share = tok_grp // blk_count
    summed_heads = lax.psum_scatter(
        jnp.dot(attn_out, out_weight, preferred_element_type=jnp.float32).astype(jnp.bfloat16),
        "blk",
        scatter_dimension=0,
        tiled=True,
    ).astype(jnp.float32)
    residual = lax.dynamic_slice_in_dim(token_values, blk_index * out_share, out_share, 0)
    return (residual + summed_heads).astype(jnp.bfloat16)


def solution(mesh):
    return jax.shard_map(
        body,
        mesh=mesh,
        in_specs=(
            P("req", None),
            P(),
            P(),
            P(None, "blk"),
            P("blk"),
            P("blk", None),
            P(),
            P(),
            P(None, "blk"),
            P("blk"),
            P(),
            P("req", "blk"),
            P("req", None),
            P(),
            P(None, "blk"),
            P(None, "blk"),
            P(None, "blk"),
            P("blk", None),
        ),
        out_specs=P(("req", "blk"), None),
        check_vma=False,
    )
```

```python
import jax
import jax.numpy as jnp
from jax import lax
from jax.sharding import PartitionSpec as P

HEAD = 128


def layer_norm(values, gain_vector, shift_vector):
    centre = jnp.mean(values, axis=-1, keepdims=True)
    centred = values - centre
    spread = jnp.mean(centred * centred, axis=-1, keepdims=True)
    result = centred * lax.rsqrt(spread + 1e-06) * gain_vector.astype(jnp.float32)
    if shift_vector is None:
        return result
    return result + shift_vector.astype(jnp.float32)


def rotate(values, positions):
    half_size = HEAD // 2
    frequency = 10000.0 ** (-2.0 * jnp.arange(half_size, dtype=jnp.float32) / HEAD)
    angles = positions.astype(jnp.float32)[:, None] * frequency[None, :]
    cosine = jnp.cos(angles)[:, None, :]
    sine_table = jnp.sin(angles)[:, None, :]
    by_head = values.reshape(values.shape[0], -1, HEAD)
    first_half = by_head[..., :half_size]
    second_half = by_head[..., half_size:]
    turned = jnp.concatenate(
        [
            first_half * cosine - second_half * sine_table,
            second_half * cosine + first_half * sine_table,
        ],
        axis=-1,
    )
    return turned.reshape(values.shape)


def causal_setup(segments):
    length = segments.shape[0]
    column_ids = jnp.arange(length)
    same_request = segments[:, None] == segments[None, :]
    earlier = column_ids[None, :] < column_ids[:, None]
    positions = jnp.sum(same_request & earlier, axis=1)
    allowed = same_request & (column_ids[None, :] <= column_ids[:, None])
    return (positions, allowed)


def attend(queries, keys, values, allowed):
    row_count = queries.shape[0]
    key_count = keys.shape[0]
    query_heads = queries.reshape(row_count, -1, HEAD)
    key_heads = keys.reshape(key_count, -1, HEAD)
    value_heads = values.reshape(key_count, -1, HEAD)
    scores = jnp.einsum(
        "thd,shd->hts", query_heads, key_heads, preferred_element_type=jnp.float32
    ) * HEAD ** (-0.5)
    scores = jnp.where(allowed[None, :, :], scores, -jnp.inf)
    top_score = jnp.max(scores, axis=-1, keepdims=True)
    weights = jnp.exp(scores - top_score)
    weights = (weights / jnp.sum(weights, axis=-1, keepdims=True)).astype(jnp.bfloat16)
    mixed = jnp.einsum("hts,shd->thd", weights, value_heads, preferred_element_type=jnp.float32)
    return mixed.astype(jnp.bfloat16).reshape(row_count, -1)


def body(
    patches,
    vis_ln_gain,
    vis_ln_bias,
    vis_up,
    vis_up_bias,
    vis_down,
    vis_down_bias,
    merge_gain,
    merge_proj,
    merge_proj_bias,
    image_dest,
    text_embed,
    segment_ids,
    text_gain,
    query_weight,
    key_weight,
    value_weight,
    out_weight,
):
    blk_count = lax.axis_size("blk")
    req_count = lax.axis_size("req")
    blk_index = lax.axis_index("blk")
    req_index = lax.axis_index("req")
    vis_width = patches.shape[1]
    gathered_text = lax.all_gather(text_embed, "blk", axis=1, tiled=True)
    patch_rows = patches.astype(jnp.float32)
    normed = layer_norm(patch_rows, vis_ln_gain, vis_ln_bias).astype(jnp.bfloat16)
    pre_act = jnp.dot(normed, vis_up, preferred_element_type=jnp.float32) + vis_up_bias.astype(
        jnp.float32
    )
    hidden = jax.nn.gelu(pre_act, approximate=False).astype(jnp.bfloat16)
    partial = jnp.dot(hidden, vis_down, preferred_element_type=jnp.float32).astype(jnp.bfloat16)
    patch_count = patches.shape[0]
    row_share = patch_count // blk_count
    parts_here = lax.all_to_all(
        partial.reshape(blk_count, row_share, vis_width), "blk", 0, 0, tiled=False
    )
    summed = jnp.sum(parts_here.astype(jnp.float32), axis=0)
    own_rows = lax.dynamic_slice_in_dim(patch_rows, blk_index * row_share, row_share, 0)
    vis_out = own_rows + summed + vis_down_bias.astype(jnp.float32)
    normed = layer_norm(vis_out, merge_gain, None).astype(jnp.bfloat16)
    merged_here = normed.reshape(-1, 4 * vis_width)
    merged_all = lax.all_to_all(
        jnp.broadcast_to(merged_here[None], (blk_count,) + merged_here.shape),
        "blk",
        0,
        0,
        tiled=False,
    )
    image_cols = jnp.dot(
        merged_all.reshape(-1, 4 * vis_width), merge_proj, preferred_element_type=jnp.float32
    )
    image_cols = (image_cols + merge_proj_bias.astype(jnp.float32)).astype(jnp.bfloat16)
    image_count = image_cols.shape[0]
    col_width = image_cols.shape[1]
    tok_grp = text_embed.shape[0]
    dest_group = image_dest // tok_grp
    dest_local = image_dest - dest_group * tok_grp
    target = jnp.where(dest_group == req_index, dest_local, tok_grp)
    filler = jnp.zeros((1, col_width), jnp.bfloat16)
    capacity = image_count // 4 + 3 * image_count // 4 // req_count
    by_source = dest_group.reshape(req_count, image_count)
    one_hot = (
        by_source[:, :, None] == jnp.arange(req_count, dtype=jnp.int32)[None, None, :]
    ).astype(jnp.int32)
    slot_index = jnp.sum((jnp.cumsum(one_hot, axis=1) - one_hot) * one_hot, axis=2)
    send_slot = lax.dynamic_index_in_dim(
        by_source * capacity + slot_index, req_index, 0, keepdims=False
    )
    source_row = (
        jnp.full((req_count * capacity,), image_count, jnp.int32)
        .at[send_slot]
        .set(jnp.arange(image_count, dtype=jnp.int32))
    )
    outgoing = jnp.take(jnp.concatenate([image_cols, filler], axis=0), source_row, axis=0)
    incoming = lax.all_to_all(outgoing, "req", split_axis=0, concat_axis=0, tiled=True)
    arrival = (jnp.arange(req_count, dtype=jnp.int32)[:, None] * capacity + slot_index).reshape(-1)
    mine = (dest_group == req_index).astype(jnp.int32)
    rank = jnp.cumsum(mine) - mine
    total_images = image_dest.shape[0]
    pick = (
        jnp.zeros((image_count,), jnp.int32)
        .at[jnp.where(mine > 0, rank, image_count)]
        .set(jnp.arange(total_images, dtype=jnp.int32), mode="drop")
    )
    mine_cols = jnp.take(incoming, jnp.take(arrival, pick), axis=0)
    mine_rows = lax.all_to_all(
        jnp.broadcast_to(mine_cols[None], (blk_count,) + mine_cols.shape), "blk", 0, 0, tiled=False
    )
    mine_rows = mine_rows.transpose(1, 0, 2).reshape(image_count, -1)
    lookup = (
        jnp.full((tok_grp,), image_count, jnp.int32)
        .at[jnp.take(dest_local, pick)]
        .set(jnp.arange(image_count, dtype=jnp.int32))
    )
    choose = (lookup[:, None] == jnp.arange(image_count, dtype=jnp.int32)[None, :]).astype(
        jnp.bfloat16
    )
    placed = jnp.dot(choose, mine_rows, preferred_element_type=jnp.float32).astype(jnp.bfloat16)
    features = jnp.where((lookup < image_count)[:, None], placed, gathered_text)
    token_values = features.astype(jnp.float32)
    normed_tokens = (
        token_values
        * lax.rsqrt(jnp.mean(token_values * token_values, axis=-1, keepdims=True) + 1e-05)
        * text_gain.astype(jnp.float32)
    ).astype(jnp.bfloat16)
    positions, allowed = causal_setup(segment_ids[0])
    head_cols = query_weight.shape[1]
    qkv_weight = jnp.concatenate([query_weight, key_weight, value_weight], axis=1)
    qkv = jnp.dot(normed_tokens, qkv_weight, preferred_element_type=jnp.float32)
    queries = rotate(qkv[:, :head_cols], positions).astype(jnp.bfloat16)
    keys_rot = rotate(qkv[:, head_cols : 2 * head_cols], positions).astype(jnp.bfloat16)
    values_here = qkv[:, 2 * head_cols :].astype(jnp.bfloat16)
    block_rows = min(512, tok_grp)
    block_count = tok_grp // block_rows

    def attend_block(block_pair):
        return attend(block_pair[0], keys_rot, values_here, block_pair[1])

    attn_out = lax.map(
        attend_block,
        (
            queries.reshape(block_count, block_rows, -1),
            allowed.reshape(block_count, block_rows, tok_grp),
        ),
    ).reshape(tok_grp, -1)
    out_share = tok_grp // blk_count
    summed_heads = lax.psum_scatter(
        jnp.dot(attn_out, out_weight, preferred_element_type=jnp.float32).astype(jnp.bfloat16),
        "blk",
        scatter_dimension=0,
        tiled=True,
    ).astype(jnp.float32)
    residual = lax.dynamic_slice_in_dim(features, blk_index * out_share, out_share, 0).astype(
        jnp.float32
    )
    return (residual + summed_heads).astype(jnp.bfloat16)


def solution(mesh):
    return jax.shard_map(
        body,
        mesh=mesh,
        in_specs=(
            P("req", None),
            P(),
            P(),
            P(None, "blk"),
            P("blk"),
            P("blk", None),
            P(),
            P(),
            P(None, "blk"),
            P("blk"),
            P(),
            P("req", "blk"),
            P("req", None),
            P(),
            P(None, "blk"),
            P(None, "blk"),
            P(None, "blk"),
            P("blk", None),
        ),
        out_specs=P(("req", "blk"), None),
        check_vma=False,
    )
```

```python
import jax
import jax.numpy as jnp
from jax import lax
from jax.sharding import Mesh, PartitionSpec as P

HEAD = 128


def layer_norm(values, gain_vector, shift_vector):
    centre = jnp.mean(values, axis=-1, keepdims=True)
    centred = values - centre
    spread = jnp.mean(centred * centred, axis=-1, keepdims=True)
    result = centred * lax.rsqrt(spread + 1e-06) * gain_vector.astype(jnp.float32)
    if shift_vector is None:
        return result
    return result + shift_vector.astype(jnp.float32)


def rotate(values, positions):
    half_size = HEAD // 2
    frequency = 10000.0 ** (-2.0 * jnp.arange(half_size, dtype=jnp.float32) / HEAD)
    angles = positions.astype(jnp.float32)[:, None] * frequency[None, :]
    cosine = jnp.cos(angles)[:, None, :]
    sine_table = jnp.sin(angles)[:, None, :]
    by_head = values.reshape(values.shape[0], -1, HEAD)
    first_half = by_head[..., :half_size]
    second_half = by_head[..., half_size:]
    turned = jnp.concatenate(
        [
            first_half * cosine - second_half * sine_table,
            second_half * cosine + first_half * sine_table,
        ],
        axis=-1,
    )
    return turned.reshape(values.shape)


def causal_setup(segments):
    length = segments.shape[0]
    column_ids = jnp.arange(length)
    same_request = segments[:, None] == segments[None, :]
    earlier = column_ids[None, :] < column_ids[:, None]
    positions = jnp.sum(same_request & earlier, axis=1)
    allowed = same_request & (column_ids[None, :] <= column_ids[:, None])
    return (positions, allowed)


def attend(queries, keys, values, allowed):
    row_count = queries.shape[0]
    key_count = keys.shape[0]
    query_heads = queries.reshape(row_count, -1, HEAD)
    key_heads = keys.reshape(key_count, -1, HEAD)
    value_heads = values.reshape(key_count, -1, HEAD)
    scores = jnp.einsum(
        "thd,shd->hts", query_heads, key_heads, preferred_element_type=jnp.float32
    ) * HEAD ** (-0.5)
    scores = jnp.where(allowed[None, :, :], scores, -jnp.inf)
    top_score = jnp.max(scores, axis=-1, keepdims=True)
    weights = jnp.exp(scores - top_score)
    weights = (weights / jnp.sum(weights, axis=-1, keepdims=True)).astype(jnp.bfloat16)
    mixed = jnp.einsum("hts,shd->thd", weights, value_heads, preferred_element_type=jnp.float32)
    return mixed.astype(jnp.bfloat16).reshape(row_count, -1)


def body(
    patches,
    vis_ln_gain,
    vis_ln_bias,
    vis_up,
    vis_up_bias,
    vis_down,
    vis_down_bias,
    merge_gain,
    merge_proj,
    merge_proj_bias,
    image_dest,
    text_embed,
    segment_ids,
    text_gain,
    query_weight,
    key_weight,
    value_weight,
    out_weight,
):
    pair_count = lax.axis_size("core")
    blk_count = lax.axis_size("xy") * pair_count
    req_count = lax.axis_size("req")
    core_index = lax.axis_index("core")
    blk_index = lax.axis_index("xy") * pair_count + core_index
    req_index = lax.axis_index("req")
    vis_width = patches.shape[1]
    gathered_text = lax.all_gather(text_embed, BLK, axis=1, tiled=True)
    partner_weight = lax.ppermute(out_weight, "core", [(0, 1), (1, 0)])
    patch_rows = patches.astype(jnp.float32)
    normed = layer_norm(patch_rows, vis_ln_gain, vis_ln_bias).astype(jnp.bfloat16)
    pre_act = jnp.dot(normed, vis_up, preferred_element_type=jnp.float32) + vis_up_bias.astype(
        jnp.float32
    )
    hidden = jax.nn.gelu(pre_act, approximate=False).astype(jnp.bfloat16)
    partial = jnp.dot(hidden, vis_down, preferred_element_type=jnp.float32).astype(jnp.bfloat16)
    patch_count = patches.shape[0]
    row_share = patch_count // blk_count
    parts_here = lax.all_to_all(
        partial.reshape(blk_count, row_share, vis_width), BLK, 0, 0, tiled=False
    )
    summed = jnp.sum(parts_here.astype(jnp.float32), axis=0)
    own_rows = lax.dynamic_slice_in_dim(patch_rows, blk_index * row_share, row_share, 0)
    vis_out = own_rows + summed + vis_down_bias.astype(jnp.float32)
    normed = layer_norm(vis_out, merge_gain, None).astype(jnp.bfloat16)
    merged_here = normed.reshape(-1, 4 * vis_width)
    merged_all = lax.all_to_all(
        jnp.broadcast_to(merged_here[None], (blk_count,) + merged_here.shape),
        BLK,
        0,
        0,
        tiled=False,
    )
    image_cols = jnp.dot(
        merged_all.reshape(-1, 4 * vis_width), merge_proj, preferred_element_type=jnp.float32
    )
    image_cols = (image_cols + merge_proj_bias.astype(jnp.float32)).astype(jnp.bfloat16)
    image_count = image_cols.shape[0]
    col_width = image_cols.shape[1]
    tok_grp = text_embed.shape[0]
    dest_group = image_dest // tok_grp
    dest_local = image_dest - dest_group * tok_grp
    target = jnp.where(dest_group == req_index, dest_local, tok_grp)
    filler = jnp.zeros((1, col_width), jnp.bfloat16)
    capacity = image_count // 4 + 3 * image_count // 4 // req_count
    by_source = dest_group.reshape(req_count, image_count)
    one_hot = (
        by_source[:, :, None] == jnp.arange(req_count, dtype=jnp.int32)[None, None, :]
    ).astype(jnp.int32)
    slot_index = jnp.sum((jnp.cumsum(one_hot, axis=1) - one_hot) * one_hot, axis=2)
    send_slot = lax.dynamic_index_in_dim(
        by_source * capacity + slot_index, req_index, 0, keepdims=False
    )
    source_row = (
        jnp.full((req_count * capacity,), image_count, jnp.int32)
        .at[send_slot]
        .set(jnp.arange(image_count, dtype=jnp.int32))
    )
    outgoing = jnp.take(jnp.concatenate([image_cols, filler], axis=0), source_row, axis=0)
    incoming = lax.all_to_all(outgoing, "req", split_axis=0, concat_axis=0, tiled=True)
    arrival = (jnp.arange(req_count, dtype=jnp.int32)[:, None] * capacity + slot_index).reshape(-1)
    mine = (dest_group == req_index).astype(jnp.int32)
    rank = jnp.cumsum(mine) - mine
    total_images = image_dest.shape[0]
    pick = (
        jnp.zeros((image_count,), jnp.int32)
        .at[jnp.where(mine > 0, rank, image_count)]
        .set(jnp.arange(total_images, dtype=jnp.int32), mode="drop")
    )
    mine_cols = jnp.take(incoming, jnp.take(arrival, pick), axis=0)
    mine_rows = lax.all_to_all(
        jnp.broadcast_to(mine_cols[None], (blk_count,) + mine_cols.shape), BLK, 0, 0, tiled=False
    )
    mine_rows = mine_rows.transpose(1, 0, 2).reshape(image_count, -1)
    lookup = (
        jnp.full((tok_grp,), image_count, jnp.int32)
        .at[jnp.take(dest_local, pick)]
        .set(jnp.arange(image_count, dtype=jnp.int32))
    )
    choose = (lookup[:, None] == jnp.arange(image_count, dtype=jnp.int32)[None, :]).astype(
        jnp.bfloat16
    )
    placed = jnp.dot(choose, mine_rows, preferred_element_type=jnp.float32).astype(jnp.bfloat16)
    features = jnp.where((lookup < image_count)[:, None], placed, gathered_text)
    token_values = features.astype(jnp.float32)
    normed_tokens = (
        token_values
        * lax.rsqrt(jnp.mean(token_values * token_values, axis=-1, keepdims=True) + 1e-05)
        * text_gain.astype(jnp.float32)
    ).astype(jnp.bfloat16)
    positions, allowed = causal_setup(segment_ids[0])
    head_cols = query_weight.shape[1]
    qkv_weight = jnp.concatenate([query_weight, key_weight, value_weight], axis=1)
    qkv = jnp.dot(normed_tokens, qkv_weight, preferred_element_type=jnp.float32)
    queries = rotate(qkv[:, :head_cols], positions).astype(jnp.bfloat16)
    keys_rot = rotate(qkv[:, head_cols : 2 * head_cols], positions).astype(jnp.bfloat16)
    values_here = qkv[:, 2 * head_cols :].astype(jnp.bfloat16)
    block_rows = min(512, tok_grp)
    block_count = tok_grp // block_rows

    def attend_block(block_pair):
        return attend(block_pair[0], keys_rot, values_here, block_pair[1])

    attn_out = lax.map(
        attend_block,
        (
            queries.reshape(block_count, block_rows, -1),
            allowed.reshape(block_count, block_rows, tok_grp),
        ),
    ).reshape(tok_grp, -1)
    out_share = tok_grp // blk_count
    swap = [(0, 1), (1, 0)]
    by_core = attn_out.reshape(blk_count // pair_count, pair_count, out_share, -1)
    attn_mine = lax.dynamic_index_in_dim(by_core, core_index, 1, keepdims=False)
    attn_other = lax.ppermute(
        lax.dynamic_index_in_dim(by_core, 1 - core_index, 1, keepdims=False), "core", swap
    )
    pair_attn = jnp.concatenate([attn_mine, attn_other], axis=-1).reshape(
        tok_grp // pair_count, -1
    )
    pair_weight = jnp.concatenate([out_weight, partner_weight], axis=0)
    pair_sum = jnp.dot(pair_attn, pair_weight, preferred_element_type=jnp.float32).astype(
        jnp.bfloat16
    )
    summed_heads = lax.psum_scatter(pair_sum, "xy", scatter_dimension=0, tiled=True).astype(
        jnp.float32
    )
    residual = lax.dynamic_slice_in_dim(features, blk_index * out_share, out_share, 0).astype(
        jnp.float32
    )
    return (residual + summed_heads).astype(jnp.bfloat16)


BLK = ("xy", "core")


def solution(mesh):
    blk_size, req_size = mesh.devices.shape
    pair_mesh = Mesh(mesh.devices.reshape(blk_size // 2, 2, req_size), ("xy", "core", "req"))
    return jax.shard_map(
        body,
        mesh=pair_mesh,
        in_specs=(
            P("req", None),
            P(),
            P(),
            P(None, BLK),
            P(BLK),
            P(BLK, None),
            P(),
            P(),
            P(None, BLK),
            P(BLK),
            P(),
            P("req", BLK),
            P("req", None),
            P(),
            P(None, BLK),
            P(None, BLK),
            P(None, BLK),
            P(BLK, None),
        ),
        out_specs=P(("req",) + BLK, None),
        check_vma=False,
    )
```

```python
import jax
import jax.numpy as jnp
from jax import lax
from jax.sharding import Mesh, PartitionSpec as P

HEAD = 128


def layer_norm(values, gain_vector, shift_vector):
    centre = jnp.mean(values, axis=-1, keepdims=True)
    centred = values - centre
    spread = jnp.mean(centred * centred, axis=-1, keepdims=True)
    result = centred * lax.rsqrt(spread + 1e-06) * gain_vector.astype(jnp.float32)
    if shift_vector is None:
        return result
    return result + shift_vector.astype(jnp.float32)


def rotate(values, positions):
    half_size = HEAD // 2
    frequency = 10000.0 ** (-2.0 * jnp.arange(half_size, dtype=jnp.float32) / HEAD)
    angles = positions.astype(jnp.float32)[:, None] * frequency[None, :]
    cosine = jnp.cos(angles)[:, None, :]
    sine_table = jnp.sin(angles)[:, None, :]
    by_head = values.reshape(values.shape[0], -1, HEAD)
    first_half = by_head[..., :half_size]
    second_half = by_head[..., half_size:]
    turned = jnp.concatenate(
        [
            first_half * cosine - second_half * sine_table,
            second_half * cosine + first_half * sine_table,
        ],
        axis=-1,
    )
    return turned.reshape(values.shape)


def causal_setup(segments):
    length = segments.shape[0]
    column_ids = jnp.arange(length)
    same_request = segments[:, None] == segments[None, :]
    earlier = column_ids[None, :] < column_ids[:, None]
    positions = jnp.sum(same_request & earlier, axis=1)
    allowed = same_request & (column_ids[None, :] <= column_ids[:, None])
    return (positions, allowed)


def attend(queries, keys, values, allowed):
    row_count = queries.shape[0]
    key_count = keys.shape[0]
    query_heads = queries.reshape(row_count, -1, HEAD)
    key_heads = keys.reshape(key_count, -1, HEAD)
    value_heads = values.reshape(key_count, -1, HEAD)
    scores = jnp.einsum(
        "thd,shd->hts", query_heads, key_heads, preferred_element_type=jnp.float32
    ) * HEAD ** (-0.5)
    scores = jnp.where(allowed[None, :, :], scores, -jnp.inf)
    top_score = jnp.max(scores, axis=-1, keepdims=True)
    weights = jnp.exp(scores - top_score)
    weights = (weights / jnp.sum(weights, axis=-1, keepdims=True)).astype(jnp.bfloat16)
    mixed = jnp.einsum("hts,shd->thd", weights, value_heads, preferred_element_type=jnp.float32)
    return mixed.astype(jnp.bfloat16).reshape(row_count, -1)


def body(
    patches,
    vis_ln_gain,
    vis_ln_bias,
    vis_up,
    vis_up_bias,
    vis_down,
    vis_down_bias,
    merge_gain,
    merge_proj,
    merge_proj_bias,
    image_dest,
    text_embed,
    segment_ids,
    text_gain,
    query_weight,
    key_weight,
    value_weight,
    out_weight,
):
    pair_count = lax.axis_size("core")
    blk_count = lax.axis_size("xy") * pair_count
    req_count = lax.axis_size("req")
    core_index = lax.axis_index("core")
    blk_index = lax.axis_index("xy") * pair_count + core_index
    req_index = lax.axis_index("req")
    vis_width = patches.shape[1]
    gathered_text = lax.all_gather(text_embed, BLK, axis=1, tiled=True)
    partner_weight = lax.ppermute(out_weight, "core", [(0, 1), (1, 0)])
    patch_rows = patches.astype(jnp.float32)
    normed = layer_norm(patch_rows, vis_ln_gain, vis_ln_bias).astype(jnp.bfloat16)
    pre_act = jnp.dot(normed, vis_up, preferred_element_type=jnp.float32) + vis_up_bias.astype(
        jnp.float32
    )
    hidden = jax.nn.gelu(pre_act, approximate=False).astype(jnp.bfloat16)
    partial = jnp.dot(hidden, vis_down, preferred_element_type=jnp.float32).astype(jnp.bfloat16)
    patch_count = patches.shape[0]
    row_share = patch_count // blk_count
    parts_here = lax.all_to_all(
        partial.reshape(blk_count, row_share, vis_width), BLK, 0, 0, tiled=False
    )
    summed = jnp.sum(parts_here.astype(jnp.float32), axis=0)
    own_rows = lax.dynamic_slice_in_dim(patch_rows, blk_index * row_share, row_share, 0)
    vis_out = own_rows + summed + vis_down_bias.astype(jnp.float32)
    normed = layer_norm(vis_out, merge_gain, None).astype(jnp.bfloat16)
    merged_here = normed.reshape(-1, 4 * vis_width)
    merged_all = lax.all_to_all(
        jnp.broadcast_to(merged_here[None], (blk_count,) + merged_here.shape),
        BLK,
        0,
        0,
        tiled=False,
    )
    image_cols = jnp.dot(
        merged_all.reshape(-1, 4 * vis_width), merge_proj, preferred_element_type=jnp.float32
    )
    image_cols = (image_cols + merge_proj_bias.astype(jnp.float32)).astype(jnp.bfloat16)
    image_count = image_cols.shape[0]
    col_width = image_cols.shape[1]
    tok_grp = text_embed.shape[0]
    dest_group = image_dest // tok_grp
    dest_local = image_dest - dest_group * tok_grp
    target = jnp.where(dest_group == req_index, dest_local, tok_grp)
    filler = jnp.zeros((1, col_width), jnp.bfloat16)
    capacity = image_count // 4 + 3 * image_count // 4 // req_count
    by_source = dest_group.reshape(req_count, image_count)
    one_hot = (
        by_source[:, :, None] == jnp.arange(req_count, dtype=jnp.int32)[None, None, :]
    ).astype(jnp.int32)
    slot_index = jnp.sum((jnp.cumsum(one_hot, axis=1) - one_hot) * one_hot, axis=2)
    send_slot = lax.dynamic_index_in_dim(
        by_source * capacity + slot_index, req_index, 0, keepdims=False
    )
    source_row = (
        jnp.full((req_count * capacity,), image_count, jnp.int32)
        .at[send_slot]
        .set(jnp.arange(image_count, dtype=jnp.int32))
    )
    outgoing = jnp.take(jnp.concatenate([image_cols, filler], axis=0), source_row, axis=0)
    incoming = lax.all_to_all(outgoing, "req", split_axis=0, concat_axis=0, tiled=True)
    arrival = (jnp.arange(req_count, dtype=jnp.int32)[:, None] * capacity + slot_index).reshape(-1)
    mine = (dest_group == req_index).astype(jnp.int32)
    rank = jnp.cumsum(mine) - mine
    total_images = image_dest.shape[0]
    pick = (
        jnp.zeros((image_count,), jnp.int32)
        .at[jnp.where(mine > 0, rank, image_count)]
        .set(jnp.arange(total_images, dtype=jnp.int32), mode="drop")
    )
    mine_cols = jnp.take(incoming, jnp.take(arrival, pick), axis=0)
    mine_rows = lax.all_to_all(
        jnp.broadcast_to(mine_cols[None], (blk_count,) + mine_cols.shape), BLK, 0, 0, tiled=False
    )
    mine_rows = mine_rows.transpose(1, 0, 2).reshape(image_count, -1)
    lookup = (
        jnp.full((tok_grp,), image_count, jnp.int32)
        .at[jnp.take(dest_local, pick)]
        .set(jnp.arange(image_count, dtype=jnp.int32))
    )
    choose = (lookup[:, None] == jnp.arange(image_count, dtype=jnp.int32)[None, :]).astype(
        jnp.bfloat16
    )
    placed = jnp.dot(choose, mine_rows, preferred_element_type=jnp.float32).astype(jnp.bfloat16)
    features = jnp.where((lookup < image_count)[:, None], placed, gathered_text)
    token_values = features.astype(jnp.float32)
    normed_tokens = (
        token_values
        * lax.rsqrt(jnp.mean(token_values * token_values, axis=-1, keepdims=True) + 1e-05)
        * text_gain.astype(jnp.float32)
    ).astype(jnp.bfloat16)
    positions, allowed = causal_setup(segment_ids[0])
    head_cols = query_weight.shape[1]
    qkv_weight = jnp.concatenate([query_weight, key_weight, value_weight], axis=1)
    qkv = jnp.dot(normed_tokens, qkv_weight, preferred_element_type=jnp.float32)
    queries = rotate(qkv[:, :head_cols], positions).astype(jnp.bfloat16)
    keys_rot = rotate(qkv[:, head_cols : 2 * head_cols], positions).astype(jnp.bfloat16)
    values_here = qkv[:, 2 * head_cols :].astype(jnp.bfloat16)
    block_rows = min(512, tok_grp)
    block_count = tok_grp // block_rows

    def attend_block(block_pair):
        return attend(block_pair[0], keys_rot, values_here, block_pair[1])

    attn_out = lax.map(
        attend_block,
        (
            queries.reshape(block_count, block_rows, -1),
            allowed.reshape(block_count, block_rows, tok_grp),
        ),
    ).reshape(tok_grp, -1)
    out_share = tok_grp // blk_count
    swap = [(0, 1), (1, 0)]
    by_core = attn_out.reshape(blk_count // pair_count, pair_count, out_share, -1)
    attn_mine = lax.dynamic_index_in_dim(by_core, core_index, 1, keepdims=False)
    attn_other = lax.ppermute(
        lax.dynamic_index_in_dim(by_core, 1 - core_index, 1, keepdims=False), "core", swap
    )
    pair_attn = jnp.concatenate([attn_mine, attn_other], axis=-1).reshape(
        tok_grp // pair_count, -1
    )
    pair_weight = jnp.concatenate([out_weight, partner_weight], axis=0)
    pair_sum = jnp.dot(pair_attn, pair_weight, preferred_element_type=jnp.float32).astype(
        jnp.bfloat16
    )
    chip_count = blk_count // pair_count
    sums_here = lax.all_to_all(
        pair_sum.reshape(chip_count, out_share, -1), "xy", 0, 0, tiled=False
    )
    summed_heads = jnp.sum(sums_here.astype(jnp.float32), axis=0)
    residual = lax.dynamic_slice_in_dim(features, blk_index * out_share, out_share, 0).astype(
        jnp.float32
    )
    return (residual + summed_heads).astype(jnp.bfloat16)


BLK = ("xy", "core")


def solution(mesh):
    blk_size, req_size = mesh.devices.shape
    pair_mesh = Mesh(mesh.devices.reshape(blk_size // 2, 2, req_size), ("xy", "core", "req"))
    return jax.shard_map(
        body,
        mesh=pair_mesh,
        in_specs=(
            P("req", None),
            P(),
            P(),
            P(None, BLK),
            P(BLK),
            P(BLK, None),
            P(),
            P(),
            P(None, BLK),
            P(BLK),
            P(),
            P("req", BLK),
            P("req", None),
            P(),
            P(None, BLK),
            P(None, BLK),
            P(None, BLK),
            P(BLK, None),
        ),
        out_specs=P(("req",) + BLK, None),
        check_vma=False,
    )
```

```python
import jax
import jax.numpy as jnp
from jax import lax
from jax.sharding import Mesh, PartitionSpec as P

HEAD = 128


def layer_norm(values, gain_vector, shift_vector):
    centre = jnp.mean(values, axis=-1, keepdims=True)
    centred = values - centre
    spread = jnp.mean(centred * centred, axis=-1, keepdims=True)
    result = centred * lax.rsqrt(spread + 1e-06) * gain_vector.astype(jnp.float32)
    if shift_vector is None:
        return result
    return result + shift_vector.astype(jnp.float32)


def rotate(values, positions):
    half_size = HEAD // 2
    frequency = 10000.0 ** (-2.0 * jnp.arange(half_size, dtype=jnp.float32) / HEAD)
    angles = positions.astype(jnp.float32)[:, None] * frequency[None, :]
    cosine = jnp.cos(angles)[:, None, :]
    sine_table = jnp.sin(angles)[:, None, :]
    by_head = values.reshape(values.shape[0], -1, HEAD)
    first_half = by_head[..., :half_size]
    second_half = by_head[..., half_size:]
    turned = jnp.concatenate(
        [
            first_half * cosine - second_half * sine_table,
            second_half * cosine + first_half * sine_table,
        ],
        axis=-1,
    )
    return turned.reshape(values.shape)


def causal_setup(segments):
    length = segments.shape[0]
    column_ids = jnp.arange(length)
    same_request = segments[:, None] == segments[None, :]
    earlier = column_ids[None, :] < column_ids[:, None]
    positions = jnp.sum(same_request & earlier, axis=1)
    allowed = same_request & (column_ids[None, :] <= column_ids[:, None])
    return (positions, allowed)


def attend(queries, keys, values, allowed):
    row_count = queries.shape[0]
    key_count = keys.shape[0]
    query_heads = queries.reshape(row_count, -1, HEAD)
    key_heads = keys.reshape(key_count, -1, HEAD)
    value_heads = values.reshape(key_count, -1, HEAD)
    scores = jnp.einsum(
        "thd,shd->hts", query_heads, key_heads, preferred_element_type=jnp.float32
    ) * HEAD ** (-0.5)
    scores = jnp.where(allowed[None, :, :], scores, -jnp.inf)
    top_score = jnp.max(scores, axis=-1, keepdims=True)
    weights = jnp.exp(scores - top_score)
    weights = (weights / jnp.sum(weights, axis=-1, keepdims=True)).astype(jnp.bfloat16)
    mixed = jnp.einsum("hts,shd->thd", weights, value_heads, preferred_element_type=jnp.float32)
    return mixed.astype(jnp.bfloat16).reshape(row_count, -1)


def body(
    patches,
    vis_ln_gain,
    vis_ln_bias,
    vis_up,
    vis_up_bias,
    vis_down,
    vis_down_bias,
    merge_gain,
    merge_proj,
    merge_proj_bias,
    image_dest,
    text_embed,
    segment_ids,
    text_gain,
    query_weight,
    key_weight,
    value_weight,
    out_weight,
):
    pair_count = lax.axis_size("quad")
    blk_count = lax.axis_size("grp") * pair_count
    req_count = lax.axis_size("req")
    core_index = lax.axis_index("quad")
    blk_index = lax.axis_index("grp") * pair_count + core_index
    req_index = lax.axis_index("req")
    vis_width = patches.shape[1]
    gathered_text = lax.all_gather(text_embed, BLK, axis=1, tiled=True)
    quad_weights = [out_weight] + [
        lax.ppermute(
            out_weight, "quad", [(j, (j + shift) % pair_count) for j in range(pair_count)]
        )
        for shift in range(1, pair_count)
    ]
    patch_rows = patches.astype(jnp.float32)
    normed = layer_norm(patch_rows, vis_ln_gain, vis_ln_bias).astype(jnp.bfloat16)
    pre_act = jnp.dot(normed, vis_up, preferred_element_type=jnp.float32) + vis_up_bias.astype(
        jnp.float32
    )
    hidden = jax.nn.gelu(pre_act, approximate=False).astype(jnp.bfloat16)
    partial = jnp.dot(hidden, vis_down, preferred_element_type=jnp.float32).astype(jnp.bfloat16)
    patch_count = patches.shape[0]
    row_share = patch_count // blk_count
    parts_here = lax.all_to_all(
        partial.reshape(blk_count, row_share, vis_width), BLK, 0, 0, tiled=False
    )
    summed = jnp.sum(parts_here.astype(jnp.float32), axis=0)
    own_rows = lax.dynamic_slice_in_dim(patch_rows, blk_index * row_share, row_share, 0)
    vis_out = own_rows + summed + vis_down_bias.astype(jnp.float32)
    normed = layer_norm(vis_out, merge_gain, None).astype(jnp.bfloat16)
    merged_here = normed.reshape(-1, 4 * vis_width)
    merged_all = lax.all_to_all(
        jnp.broadcast_to(merged_here[None], (blk_count,) + merged_here.shape),
        BLK,
        0,
        0,
        tiled=False,
    )
    image_cols = jnp.dot(
        merged_all.reshape(-1, 4 * vis_width), merge_proj, preferred_element_type=jnp.float32
    )
    image_cols = (image_cols + merge_proj_bias.astype(jnp.float32)).astype(jnp.bfloat16)
    image_count = image_cols.shape[0]
    col_width = image_cols.shape[1]
    tok_grp = text_embed.shape[0]
    dest_group = image_dest // tok_grp
    dest_local = image_dest - dest_group * tok_grp
    target = jnp.where(dest_group == req_index, dest_local, tok_grp)
    filler = jnp.zeros((1, col_width), jnp.bfloat16)
    capacity = image_count // 4 + 3 * image_count // 4 // req_count
    by_source = dest_group.reshape(req_count, image_count)
    one_hot = (
        by_source[:, :, None] == jnp.arange(req_count, dtype=jnp.int32)[None, None, :]
    ).astype(jnp.int32)
    slot_index = jnp.sum((jnp.cumsum(one_hot, axis=1) - one_hot) * one_hot, axis=2)
    send_slot = lax.dynamic_index_in_dim(
        by_source * capacity + slot_index, req_index, 0, keepdims=False
    )
    source_row = (
        jnp.full((req_count * capacity,), image_count, jnp.int32)
        .at[send_slot]
        .set(jnp.arange(image_count, dtype=jnp.int32))
    )
    outgoing = jnp.take(jnp.concatenate([image_cols, filler], axis=0), source_row, axis=0)
    incoming = lax.all_to_all(outgoing, "req", split_axis=0, concat_axis=0, tiled=True)
    arrival = (jnp.arange(req_count, dtype=jnp.int32)[:, None] * capacity + slot_index).reshape(-1)
    mine = (dest_group == req_index).astype(jnp.int32)
    rank = jnp.cumsum(mine) - mine
    total_images = image_dest.shape[0]
    pick = (
        jnp.zeros((image_count,), jnp.int32)
        .at[jnp.where(mine > 0, rank, image_count)]
        .set(jnp.arange(total_images, dtype=jnp.int32), mode="drop")
    )
    mine_cols = jnp.take(incoming, jnp.take(arrival, pick), axis=0)
    mine_rows = lax.all_to_all(
        jnp.broadcast_to(mine_cols[None], (blk_count,) + mine_cols.shape), BLK, 0, 0, tiled=False
    )
    mine_rows = mine_rows.transpose(1, 0, 2).reshape(image_count, -1)
    lookup = (
        jnp.full((tok_grp,), image_count, jnp.int32)
        .at[jnp.take(dest_local, pick)]
        .set(jnp.arange(image_count, dtype=jnp.int32))
    )
    choose = (lookup[:, None] == jnp.arange(image_count, dtype=jnp.int32)[None, :]).astype(
        jnp.bfloat16
    )
    placed = jnp.dot(choose, mine_rows, preferred_element_type=jnp.float32).astype(jnp.bfloat16)
    features = jnp.where((lookup < image_count)[:, None], placed, gathered_text)
    token_values = features.astype(jnp.float32)
    normed_tokens = (
        token_values
        * lax.rsqrt(jnp.mean(token_values * token_values, axis=-1, keepdims=True) + 1e-05)
        * text_gain.astype(jnp.float32)
    ).astype(jnp.bfloat16)
    positions, allowed = causal_setup(segment_ids[0])
    head_cols = query_weight.shape[1]
    qkv_weight = jnp.concatenate([query_weight, key_weight, value_weight], axis=1)
    qkv = jnp.dot(normed_tokens, qkv_weight, preferred_element_type=jnp.float32)
    queries = rotate(qkv[:, :head_cols], positions).astype(jnp.bfloat16)
    keys_rot = rotate(qkv[:, head_cols : 2 * head_cols], positions).astype(jnp.bfloat16)
    values_here = qkv[:, 2 * head_cols :].astype(jnp.bfloat16)
    block_rows = min(512, tok_grp)
    block_count = tok_grp // block_rows

    def attend_block(block_pair):
        return attend(block_pair[0], keys_rot, values_here, block_pair[1])

    attn_out = lax.map(
        attend_block,
        (
            queries.reshape(block_count, block_rows, -1),
            allowed.reshape(block_count, block_rows, tok_grp),
        ),
    ).reshape(tok_grp, -1)
    out_share = tok_grp // blk_count
    by_core = attn_out.reshape(blk_count // pair_count, pair_count, out_share, -1)
    from_quad = lax.all_to_all(by_core.transpose(1, 0, 2, 3), "quad", 0, 0, tiled=False)
    sources = (core_index - jnp.arange(pair_count, dtype=jnp.int32)) % pair_count
    in_order = jnp.take(from_quad, sources, axis=0)
    pair_attn = in_order.transpose(1, 2, 0, 3).reshape(tok_grp // pair_count, -1)
    pair_weight = jnp.concatenate(quad_weights, axis=0)
    pair_sum = jnp.dot(pair_attn, pair_weight, preferred_element_type=jnp.float32).astype(
        jnp.bfloat16
    )
    chip_count = blk_count // pair_count
    sums_here = lax.all_to_all(
        pair_sum.reshape(chip_count, out_share, -1), "grp", 0, 0, tiled=False
    )
    summed_heads = jnp.sum(sums_here.astype(jnp.float32), axis=0)
    residual = lax.dynamic_slice_in_dim(features, blk_index * out_share, out_share, 0).astype(
        jnp.float32
    )
    return (residual + summed_heads).astype(jnp.bfloat16)


BLK = ("grp", "quad")


def solution(mesh):
    blk_size, req_size = mesh.devices.shape
    pair_mesh = Mesh(mesh.devices.reshape(blk_size // 4, 4, req_size), ("grp", "quad", "req"))
    return jax.shard_map(
        body,
        mesh=pair_mesh,
        in_specs=(
            P("req", None),
            P(),
            P(),
            P(None, BLK),
            P(BLK),
            P(BLK, None),
            P(),
            P(),
            P(None, BLK),
            P(BLK),
            P(),
            P("req", BLK),
            P("req", None),
            P(),
            P(None, BLK),
            P(None, BLK),
            P(None, BLK),
            P(BLK, None),
        ),
        out_specs=P(("req",) + BLK, None),
        check_vma=False,
    )
```

```python
import jax
import jax.numpy as jnp
from jax import lax
from jax.sharding import Mesh, PartitionSpec as P

HEAD = 128


def layer_norm(values, gain_vector, shift_vector):
    centre = jnp.mean(values, axis=-1, keepdims=True)
    centred = values - centre
    spread = jnp.mean(centred * centred, axis=-1, keepdims=True)
    result = centred * lax.rsqrt(spread + 1e-06) * gain_vector.astype(jnp.float32)
    if shift_vector is None:
        return result
    return result + shift_vector.astype(jnp.float32)


def rotate(values, positions):
    half_size = HEAD // 2
    frequency = 10000.0 ** (-2.0 * jnp.arange(half_size, dtype=jnp.float32) / HEAD)
    angles = positions.astype(jnp.float32)[:, None] * frequency[None, :]
    cosine = jnp.cos(angles)[:, None, :]
    sine_table = jnp.sin(angles)[:, None, :]
    by_head = values.reshape(values.shape[0], -1, HEAD)
    first_half = by_head[..., :half_size]
    second_half = by_head[..., half_size:]
    turned = jnp.concatenate(
        [
            first_half * cosine - second_half * sine_table,
            second_half * cosine + first_half * sine_table,
        ],
        axis=-1,
    )
    return turned.reshape(values.shape)


def causal_setup(segments):
    length = segments.shape[0]
    column_ids = jnp.arange(length)
    same_request = segments[:, None] == segments[None, :]
    earlier = column_ids[None, :] < column_ids[:, None]
    positions = jnp.sum(same_request & earlier, axis=1)
    allowed = same_request & (column_ids[None, :] <= column_ids[:, None])
    return (positions, allowed)


def attend(queries, keys, values, allowed):
    row_count = queries.shape[0]
    key_count = keys.shape[0]
    query_heads = queries.reshape(row_count, -1, HEAD)
    key_heads = keys.reshape(key_count, -1, HEAD)
    value_heads = values.reshape(key_count, -1, HEAD)
    scores = jnp.einsum(
        "thd,shd->hts", query_heads, key_heads, preferred_element_type=jnp.float32
    ) * HEAD ** (-0.5)
    scores = jnp.where(allowed[None, :, :], scores, -jnp.inf)
    top_score = jnp.max(scores, axis=-1, keepdims=True)
    weights = jnp.exp(scores - top_score)
    weights = (weights / jnp.sum(weights, axis=-1, keepdims=True)).astype(jnp.bfloat16)
    mixed = jnp.einsum("hts,shd->thd", weights, value_heads, preferred_element_type=jnp.float32)
    return mixed.astype(jnp.bfloat16).reshape(row_count, -1)


def body(
    patches,
    vis_ln_gain,
    vis_ln_bias,
    vis_up,
    vis_up_bias,
    vis_down,
    vis_down_bias,
    merge_gain,
    merge_proj,
    merge_proj_bias,
    image_dest,
    text_embed,
    segment_ids,
    text_gain,
    query_weight,
    key_weight,
    value_weight,
    out_weight,
):
    pair_count = lax.axis_size("quad")
    blk_count = lax.axis_size("grp") * pair_count
    req_count = lax.axis_size("req")
    core_index = lax.axis_index("quad")
    blk_index = lax.axis_index("grp") * pair_count + core_index
    req_index = lax.axis_index("req")
    vis_width = patches.shape[1]
    gathered_text = lax.all_gather(text_embed, BLK, axis=1, tiled=True)
    quad_weights = [out_weight] + [
        lax.ppermute(
            out_weight, "quad", [(j, (j + shift) % pair_count) for j in range(pair_count)]
        )
        for shift in range(1, pair_count)
    ]
    patch_rows = patches.astype(jnp.float32)
    normed = layer_norm(patch_rows, vis_ln_gain, vis_ln_bias).astype(jnp.bfloat16)
    pre_act = jnp.dot(normed, vis_up, preferred_element_type=jnp.float32) + vis_up_bias.astype(
        jnp.float32
    )
    hidden = jax.nn.gelu(pre_act, approximate=False).astype(jnp.bfloat16)
    partial = jnp.dot(hidden, vis_down, preferred_element_type=jnp.float32).astype(jnp.bfloat16)
    patch_count = patches.shape[0]
    row_share = patch_count // blk_count
    parts_here = lax.all_to_all(
        partial.reshape(blk_count, row_share, vis_width), BLK, 0, 0, tiled=False
    )
    summed = jnp.sum(parts_here.astype(jnp.float32), axis=0)
    own_rows = lax.dynamic_slice_in_dim(patch_rows, blk_index * row_share, row_share, 0)
    vis_out = own_rows + summed + vis_down_bias.astype(jnp.float32)
    normed = layer_norm(vis_out, merge_gain, None).astype(jnp.bfloat16)
    merged_here = normed.reshape(-1, 4 * vis_width)
    merged_all = lax.all_to_all(
        jnp.broadcast_to(merged_here[None], (blk_count,) + merged_here.shape),
        BLK,
        0,
        0,
        tiled=False,
    )
    image_cols = jnp.dot(
        merged_all.reshape(-1, 4 * vis_width), merge_proj, preferred_element_type=jnp.float32
    )
    image_cols = (image_cols + merge_proj_bias.astype(jnp.float32)).astype(jnp.bfloat16)
    image_count = image_cols.shape[0]
    col_width = image_cols.shape[1]
    tok_grp = text_embed.shape[0]
    dest_group = image_dest // tok_grp
    dest_local = image_dest - dest_group * tok_grp
    target = jnp.where(dest_group == req_index, dest_local, tok_grp)
    filler = jnp.zeros((1, col_width), jnp.bfloat16)
    capacity = image_count // 4 + 3 * image_count // 4 // req_count
    by_source = dest_group.reshape(req_count, image_count)
    one_hot = (
        by_source[:, :, None] == jnp.arange(req_count, dtype=jnp.int32)[None, None, :]
    ).astype(jnp.int32)
    slot_index = jnp.sum((jnp.cumsum(one_hot, axis=1) - one_hot) * one_hot, axis=2)
    send_slot = lax.dynamic_index_in_dim(
        by_source * capacity + slot_index, req_index, 0, keepdims=False
    )
    source_row = (
        jnp.full((req_count * capacity,), image_count, jnp.int32)
        .at[send_slot]
        .set(jnp.arange(image_count, dtype=jnp.int32))
    )
    outgoing = jnp.take(jnp.concatenate([image_cols, filler], axis=0), source_row, axis=0)
    incoming = lax.all_to_all(outgoing, "req", split_axis=0, concat_axis=0, tiled=True)
    arrival = (jnp.arange(req_count, dtype=jnp.int32)[:, None] * capacity + slot_index).reshape(-1)
    mine = (dest_group == req_index).astype(jnp.int32)
    rank = jnp.cumsum(mine) - mine
    total_images = image_dest.shape[0]
    pick = (
        jnp.zeros((image_count,), jnp.int32)
        .at[jnp.where(mine > 0, rank, image_count)]
        .set(jnp.arange(total_images, dtype=jnp.int32), mode="drop")
    )
    mine_cols = jnp.take(incoming, jnp.take(arrival, pick), axis=0)
    mine_rows = lax.all_to_all(
        jnp.broadcast_to(mine_cols[None], (blk_count,) + mine_cols.shape), BLK, 0, 0, tiled=False
    )
    mine_rows = mine_rows.transpose(1, 0, 2).reshape(image_count, -1)
    lookup = (
        jnp.full((tok_grp,), image_count, jnp.int32)
        .at[jnp.take(dest_local, pick)]
        .set(jnp.arange(image_count, dtype=jnp.int32))
    )
    choose = (lookup[:, None] == jnp.arange(image_count, dtype=jnp.int32)[None, :]).astype(
        jnp.bfloat16
    )
    placed = jnp.dot(choose, mine_rows, preferred_element_type=jnp.float32).astype(jnp.bfloat16)
    features = jnp.where((lookup < image_count)[:, None], placed, gathered_text)
    token_values = features.astype(jnp.float32)
    normed_tokens = (
        token_values
        * lax.rsqrt(jnp.mean(token_values * token_values, axis=-1, keepdims=True) + 1e-05)
        * text_gain.astype(jnp.float32)
    ).astype(jnp.bfloat16)
    positions, allowed = causal_setup(segment_ids[0])
    head_cols = query_weight.shape[1]
    qkv_weight = jnp.concatenate([query_weight, key_weight, value_weight], axis=1)
    qkv = jnp.dot(normed_tokens, qkv_weight, preferred_element_type=jnp.float32)
    queries = rotate(qkv[:, :head_cols], positions).astype(jnp.bfloat16)
    keys_rot = rotate(qkv[:, head_cols : 2 * head_cols], positions).astype(jnp.bfloat16)
    values_here = qkv[:, 2 * head_cols :].astype(jnp.bfloat16)
    block_rows = min(512, tok_grp)
    block_count = tok_grp // block_rows

    def attend_block(block_pair):
        return attend(block_pair[0], keys_rot, values_here, block_pair[1])

    attn_out = lax.map(
        attend_block,
        (
            queries.reshape(block_count, block_rows, -1),
            allowed.reshape(block_count, block_rows, tok_grp),
        ),
    ).reshape(tok_grp, -1)
    out_share = tok_grp // blk_count
    by_core = attn_out.reshape(blk_count // pair_count, pair_count, out_share, -1)
    in_order = jnp.stack(
        [lax.dynamic_index_in_dim(by_core, core_index, 1, keepdims=False)]
        + [
            lax.ppermute(
                lax.dynamic_index_in_dim(
                    by_core, (core_index + shift) % pair_count, 1, keepdims=False
                ),
                "quad",
                [(j, (j + shift) % pair_count) for j in range(pair_count)],
            )
            for shift in range(1, pair_count)
        ]
    )
    pair_attn = in_order.transpose(1, 2, 0, 3).reshape(tok_grp // pair_count, -1)
    pair_weight = jnp.concatenate(quad_weights, axis=0)
    pair_sum = jnp.dot(pair_attn, pair_weight, preferred_element_type=jnp.float32).astype(
        jnp.bfloat16
    )
    chip_count = blk_count // pair_count
    sums_here = lax.all_to_all(
        pair_sum.reshape(chip_count, out_share, -1), "grp", 0, 0, tiled=False
    )
    summed_heads = jnp.sum(sums_here.astype(jnp.float32), axis=0)
    residual = lax.dynamic_slice_in_dim(features, blk_index * out_share, out_share, 0).astype(
        jnp.float32
    )
    return (residual + summed_heads).astype(jnp.bfloat16)


BLK = ("grp", "quad")


def solution(mesh):
    blk_size, req_size = mesh.devices.shape
    pair_mesh = Mesh(mesh.devices.reshape(blk_size // 4, 4, req_size), ("grp", "quad", "req"))
    return jax.shard_map(
        body,
        mesh=pair_mesh,
        in_specs=(
            P("req", None),
            P(),
            P(),
            P(None, BLK),
            P(BLK),
            P(BLK, None),
            P(),
            P(),
            P(None, BLK),
            P(BLK),
            P(),
            P("req", BLK),
            P("req", None),
            P(),
            P(None, BLK),
            P(None, BLK),
            P(None, BLK),
            P(BLK, None),
        ),
        out_specs=P(("req",) + BLK, None),
        check_vma=False,
    )
```

```python
import jax
import jax.numpy as jnp
from jax import lax
from jax.sharding import Mesh, PartitionSpec as P

HEAD = 128


def layer_norm(values, gain_vector, shift_vector):
    centre = jnp.mean(values, axis=-1, keepdims=True)
    centred = values - centre
    spread = jnp.mean(centred * centred, axis=-1, keepdims=True)
    result = centred * lax.rsqrt(spread + 1e-06) * gain_vector.astype(jnp.float32)
    if shift_vector is None:
        return result
    return result + shift_vector.astype(jnp.float32)


def rotate(values, positions):
    half_size = HEAD // 2
    frequency = 10000.0 ** (-2.0 * jnp.arange(half_size, dtype=jnp.float32) / HEAD)
    angles = positions.astype(jnp.float32)[:, None] * frequency[None, :]
    cosine = jnp.cos(angles)[:, None, :]
    sine_table = jnp.sin(angles)[:, None, :]
    by_head = values.reshape(values.shape[0], -1, HEAD)
    first_half = by_head[..., :half_size]
    second_half = by_head[..., half_size:]
    turned = jnp.concatenate(
        [
            first_half * cosine - second_half * sine_table,
            second_half * cosine + first_half * sine_table,
        ],
        axis=-1,
    )
    return turned.reshape(values.shape)


def causal_setup(segments):
    length = segments.shape[0]
    column_ids = jnp.arange(length)
    same_request = segments[:, None] == segments[None, :]
    earlier = column_ids[None, :] < column_ids[:, None]
    positions = jnp.sum(same_request & earlier, axis=1)
    allowed = same_request & (column_ids[None, :] <= column_ids[:, None])
    return (positions, allowed)


def attend(queries, keys, values, allowed):
    row_count = queries.shape[0]
    key_count = keys.shape[0]
    query_heads = queries.reshape(row_count, -1, HEAD)
    key_heads = keys.reshape(key_count, -1, HEAD)
    value_heads = values.reshape(key_count, -1, HEAD)
    scores = jnp.einsum(
        "thd,shd->hts", query_heads, key_heads, preferred_element_type=jnp.float32
    ) * HEAD ** (-0.5)
    scores = jnp.where(allowed[None, :, :], scores, -jnp.inf)
    top_score = jnp.max(scores, axis=-1, keepdims=True)
    weights = jnp.exp(scores - top_score)
    weights = (weights / jnp.sum(weights, axis=-1, keepdims=True)).astype(jnp.bfloat16)
    mixed = jnp.einsum("hts,shd->thd", weights, value_heads, preferred_element_type=jnp.float32)
    return mixed.astype(jnp.bfloat16).reshape(row_count, -1)


def body(
    patches,
    vis_ln_gain,
    vis_ln_bias,
    vis_up,
    vis_up_bias,
    vis_down,
    vis_down_bias,
    merge_gain,
    merge_proj,
    merge_proj_bias,
    image_dest,
    text_embed,
    segment_ids,
    text_gain,
    query_weight,
    key_weight,
    value_weight,
    out_weight,
):
    pair_count = lax.axis_size("quad")
    blk_count = lax.axis_size("grp") * pair_count
    req_count = lax.axis_size("req")
    core_index = lax.axis_index("quad")
    blk_index = lax.axis_index("grp") * pair_count + core_index
    req_index = lax.axis_index("req")
    vis_width = patches.shape[1]
    gathered_text = lax.all_gather(text_embed, BLK, axis=1, tiled=True)
    quad_weights = [out_weight] + [
        lax.ppermute(
            out_weight, "quad", [(j, (j + shift) % pair_count) for j in range(pair_count)]
        )
        for shift in range(1, pair_count)
    ]
    patch_rows = patches.astype(jnp.float32)
    normed = layer_norm(patch_rows, vis_ln_gain, vis_ln_bias).astype(jnp.bfloat16)
    pre_act = jnp.dot(normed, vis_up, preferred_element_type=jnp.float32) + vis_up_bias.astype(
        jnp.float32
    )
    hidden = jax.nn.gelu(pre_act, approximate=False).astype(jnp.bfloat16)
    partial = jnp.dot(hidden, vis_down, preferred_element_type=jnp.float32).astype(jnp.bfloat16)
    patch_count = patches.shape[0]
    row_share = patch_count // blk_count
    parts_here = lax.all_to_all(
        partial.reshape(blk_count, row_share, vis_width), BLK, 0, 0, tiled=False
    )
    summed = jnp.sum(parts_here.astype(jnp.float32), axis=0)
    own_rows = lax.dynamic_slice_in_dim(patch_rows, blk_index * row_share, row_share, 0)
    vis_out = own_rows + summed + vis_down_bias.astype(jnp.float32)
    normed = layer_norm(vis_out, merge_gain, None).astype(jnp.bfloat16)
    merged_here = normed.reshape(-1, 4 * vis_width)
    merged_all = lax.all_to_all(
        jnp.broadcast_to(merged_here[None], (blk_count,) + merged_here.shape),
        BLK,
        0,
        0,
        tiled=False,
    )
    image_cols = jnp.dot(
        merged_all.reshape(-1, 4 * vis_width), merge_proj, preferred_element_type=jnp.float32
    )
    image_cols = (image_cols + merge_proj_bias.astype(jnp.float32)).astype(jnp.bfloat16)
    image_count = image_cols.shape[0]
    col_width = image_cols.shape[1]
    tok_grp = text_embed.shape[0]
    dest_group = image_dest // tok_grp
    dest_local = image_dest - dest_group * tok_grp
    target = jnp.where(dest_group == req_index, dest_local, tok_grp)
    filler = jnp.zeros((1, col_width), jnp.bfloat16)
    capacity = image_count // 4 + 3 * image_count // 4 // req_count
    by_source = dest_group.reshape(req_count, image_count)
    one_hot = (
        by_source[:, :, None] == jnp.arange(req_count, dtype=jnp.int32)[None, None, :]
    ).astype(jnp.int32)
    slot_index = jnp.sum((jnp.cumsum(one_hot, axis=1) - one_hot) * one_hot, axis=2)
    send_slot = lax.dynamic_index_in_dim(
        by_source * capacity + slot_index, req_index, 0, keepdims=False
    )
    source_row = (
        jnp.full((req_count * capacity,), image_count, jnp.int32)
        .at[send_slot]
        .set(jnp.arange(image_count, dtype=jnp.int32))
    )
    outgoing = jnp.take(jnp.concatenate([image_cols, filler], axis=0), source_row, axis=0)
    incoming = lax.all_to_all(outgoing, "req", split_axis=0, concat_axis=0, tiled=True)
    arrival = (jnp.arange(req_count, dtype=jnp.int32)[:, None] * capacity + slot_index).reshape(-1)
    mine = (dest_group == req_index).astype(jnp.int32)
    rank = jnp.cumsum(mine) - mine
    total_images = image_dest.shape[0]
    pick = (
        jnp.zeros((image_count,), jnp.int32)
        .at[jnp.where(mine > 0, rank, image_count)]
        .set(jnp.arange(total_images, dtype=jnp.int32), mode="drop")
    )
    mine_cols = jnp.take(incoming, jnp.take(arrival, pick), axis=0)
    mine_rows = lax.all_to_all(
        jnp.broadcast_to(mine_cols[None], (blk_count,) + mine_cols.shape), BLK, 0, 0, tiled=False
    )
    mine_rows = mine_rows.transpose(1, 0, 2).reshape(image_count, -1)
    lookup = (
        jnp.full((tok_grp,), image_count, jnp.int32)
        .at[jnp.take(dest_local, pick)]
        .set(jnp.arange(image_count, dtype=jnp.int32))
    )
    def rms_normed(rows):
        row_values = rows.astype(jnp.float32)
        return (
            row_values
            * lax.rsqrt(jnp.mean(row_values * row_values, axis=-1, keepdims=True) + 1e-05)
            * text_gain.astype(jnp.float32)
        ).astype(jnp.bfloat16)

    positions, allowed = causal_setup(segment_ids[0])
    head_cols = query_weight.shape[1]
    qkv_weight = jnp.concatenate([query_weight, key_weight, value_weight], axis=1)
    qkv_text = jnp.dot(rms_normed(gathered_text), qkv_weight, preferred_element_type=jnp.float32)
    qkv_image = jnp.dot(rms_normed(mine_rows), qkv_weight, preferred_element_type=jnp.float32)
    is_image = (lookup < image_count)[:, None]
    qkv_table = jnp.concatenate([qkv_image, jnp.zeros_like(qkv_image[:1])], axis=0)
    qkv = jnp.where(is_image, jnp.take(qkv_table, lookup, axis=0), qkv_text)
    queries = rotate(qkv[:, :head_cols], positions).astype(jnp.bfloat16)
    keys_rot = rotate(qkv[:, head_cols : 2 * head_cols], positions).astype(jnp.bfloat16)
    values_here = qkv[:, 2 * head_cols :].astype(jnp.bfloat16)
    block_rows = min(512, tok_grp)
    block_count = tok_grp // block_rows

    def attend_block(block_pair):
        return attend(block_pair[0], keys_rot, values_here, block_pair[1])

    attn_out = lax.map(
        attend_block,
        (
            queries.reshape(block_count, block_rows, -1),
            allowed.reshape(block_count, block_rows, tok_grp),
        ),
    ).reshape(tok_grp, -1)
    out_share = tok_grp // blk_count
    by_core = attn_out.reshape(blk_count // pair_count, pair_count, out_share, -1)
    from_quad = lax.all_to_all(by_core.transpose(1, 0, 2, 3), "quad", 0, 0, tiled=False)
    sources = (core_index - jnp.arange(pair_count, dtype=jnp.int32)) % pair_count
    in_order = jnp.take(from_quad, sources, axis=0)
    pair_attn = in_order.transpose(1, 2, 0, 3).reshape(tok_grp // pair_count, -1)
    pair_weight = jnp.concatenate(quad_weights, axis=0)
    pair_sum = jnp.dot(pair_attn, pair_weight, preferred_element_type=jnp.float32).astype(
        jnp.bfloat16
    )
    chip_count = blk_count // pair_count
    sums_here = lax.all_to_all(
        pair_sum.reshape(chip_count, out_share, -1), "grp", 0, 0, tiled=False
    )
    summed_heads = jnp.sum(sums_here.astype(jnp.float32), axis=0)
    own_lookup = lax.dynamic_slice_in_dim(lookup, blk_index * out_share, out_share, 0)
    image_table = jnp.concatenate([mine_rows, jnp.zeros_like(mine_rows[:1])], axis=0)
    residual = jnp.where(
        (own_lookup < image_count)[:, None],
        jnp.take(image_table, own_lookup, axis=0),
        lax.dynamic_slice_in_dim(gathered_text, blk_index * out_share, out_share, 0),
    ).astype(jnp.float32)
    return (residual + summed_heads).astype(jnp.bfloat16)


BLK = ("grp", "quad")


def solution(mesh):
    blk_size, req_size = mesh.devices.shape
    pair_mesh = Mesh(mesh.devices.reshape(blk_size // 4, 4, req_size), ("grp", "quad", "req"))
    return jax.shard_map(
        body,
        mesh=pair_mesh,
        in_specs=(
            P("req", None),
            P(),
            P(),
            P(None, BLK),
            P(BLK),
            P(BLK, None),
            P(),
            P(),
            P(None, BLK),
            P(BLK),
            P(),
            P("req", BLK),
            P("req", None),
            P(),
            P(None, BLK),
            P(None, BLK),
            P(None, BLK),
            P(BLK, None),
        ),
        out_specs=P(("req",) + BLK, None),
        check_vma=False,
    )
```

```python
import jax
import jax.numpy as jnp
from jax import lax
from jax.sharding import Mesh, PartitionSpec as P

HEAD = 128


def layer_norm(values, gain_vector, shift_vector):
    centre = jnp.mean(values, axis=-1, keepdims=True)
    centred = values - centre
    spread = jnp.mean(centred * centred, axis=-1, keepdims=True)
    result = centred * lax.rsqrt(spread + 1e-06) * gain_vector.astype(jnp.float32)
    if shift_vector is None:
        return result
    return result + shift_vector.astype(jnp.float32)


def rotate(values, positions):
    half_size = HEAD // 2
    frequency = 10000.0 ** (-2.0 * jnp.arange(half_size, dtype=jnp.float32) / HEAD)
    angles = positions.astype(jnp.float32)[:, None] * frequency[None, :]
    cosine = jnp.cos(angles)[:, None, :]
    sine_table = jnp.sin(angles)[:, None, :]
    by_head = values.reshape(values.shape[0], -1, HEAD)
    first_half = by_head[..., :half_size]
    second_half = by_head[..., half_size:]
    turned = jnp.concatenate(
        [
            first_half * cosine - second_half * sine_table,
            second_half * cosine + first_half * sine_table,
        ],
        axis=-1,
    )
    return turned.reshape(values.shape)


def causal_setup(segments):
    length = segments.shape[0]
    column_ids = jnp.arange(length)
    same_request = segments[:, None] == segments[None, :]
    earlier = column_ids[None, :] < column_ids[:, None]
    positions = jnp.sum(same_request & earlier, axis=1)
    allowed = same_request & (column_ids[None, :] <= column_ids[:, None])
    return (positions, allowed)


def attend(queries, keys, values, allowed):
    row_count = queries.shape[0]
    key_count = keys.shape[0]
    query_heads = queries.reshape(row_count, -1, HEAD)
    key_heads = keys.reshape(key_count, -1, HEAD)
    value_heads = values.reshape(key_count, -1, HEAD)
    scores = jnp.einsum(
        "thd,shd->hts", query_heads, key_heads, preferred_element_type=jnp.float32
    ) * HEAD ** (-0.5)
    scores = jnp.where(allowed[None, :, :], scores, -jnp.inf)
    top_score = jnp.max(scores, axis=-1, keepdims=True)
    weights = jnp.exp(scores - top_score)
    weights = (weights / jnp.sum(weights, axis=-1, keepdims=True)).astype(jnp.bfloat16)
    mixed = jnp.einsum("hts,shd->thd", weights, value_heads, preferred_element_type=jnp.float32)
    return mixed.astype(jnp.bfloat16).reshape(row_count, -1)


def body(
    patches,
    vis_ln_gain,
    vis_ln_bias,
    vis_up,
    vis_up_bias,
    vis_down,
    vis_down_bias,
    merge_gain,
    merge_proj,
    merge_proj_bias,
    image_dest,
    text_embed,
    segment_ids,
    text_gain,
    query_weight,
    key_weight,
    value_weight,
    out_weight,
):
    pair_count = lax.axis_size("quad")
    blk_count = lax.axis_size("grp") * pair_count
    req_count = lax.axis_size("req")
    core_index = lax.axis_index("quad")
    blk_index = lax.axis_index("grp") * pair_count + core_index
    req_index = lax.axis_index("req")
    vis_width = patches.shape[1]
    quad_weights = [out_weight] + [
        lax.ppermute(
            out_weight, "quad", [(j, (j + shift) % pair_count) for j in range(pair_count)]
        )
        for shift in range(1, pair_count)
    ]
    patch_rows = patches.astype(jnp.float32)
    normed = layer_norm(patch_rows, vis_ln_gain, vis_ln_bias).astype(jnp.bfloat16)
    pre_act = jnp.dot(normed, vis_up, preferred_element_type=jnp.float32) + vis_up_bias.astype(
        jnp.float32
    )
    hidden = jax.nn.gelu(pre_act, approximate=False).astype(jnp.bfloat16)
    partial = jnp.dot(hidden, vis_down, preferred_element_type=jnp.float32).astype(jnp.bfloat16)
    patch_count = patches.shape[0]
    row_share = patch_count // blk_count
    parts_here = lax.all_to_all(
        partial.reshape(blk_count, row_share, vis_width), BLK, 0, 0, tiled=False
    )
    summed = jnp.sum(parts_here.astype(jnp.float32), axis=0)
    own_rows = lax.dynamic_slice_in_dim(patch_rows, blk_index * row_share, row_share, 0)
    vis_out = own_rows + summed + vis_down_bias.astype(jnp.float32)
    normed = layer_norm(vis_out, merge_gain, None).astype(jnp.bfloat16)
    merged_here = normed.reshape(-1, 4 * vis_width)
    merged_all = lax.all_to_all(
        jnp.broadcast_to(merged_here[None], (blk_count,) + merged_here.shape),
        BLK,
        0,
        0,
        tiled=False,
    )
    late_text, merged_all = lax.optimization_barrier((text_embed, merged_all))
    gathered_text = lax.all_gather(late_text, BLK, axis=1, tiled=True)
    image_cols = jnp.dot(
        merged_all.reshape(-1, 4 * vis_width), merge_proj, preferred_element_type=jnp.float32
    )
    image_cols = (image_cols + merge_proj_bias.astype(jnp.float32)).astype(jnp.bfloat16)
    image_count = image_cols.shape[0]
    col_width = image_cols.shape[1]
    tok_grp = text_embed.shape[0]
    dest_group = image_dest // tok_grp
    dest_local = image_dest - dest_group * tok_grp
    target = jnp.where(dest_group == req_index, dest_local, tok_grp)
    filler = jnp.zeros((1, col_width), jnp.bfloat16)
    capacity = image_count // 4 + 3 * image_count // 4 // req_count
    by_source = dest_group.reshape(req_count, image_count)
    one_hot = (
        by_source[:, :, None] == jnp.arange(req_count, dtype=jnp.int32)[None, None, :]
    ).astype(jnp.int32)
    slot_index = jnp.sum((jnp.cumsum(one_hot, axis=1) - one_hot) * one_hot, axis=2)
    send_slot = lax.dynamic_index_in_dim(
        by_source * capacity + slot_index, req_index, 0, keepdims=False
    )
    source_row = (
        jnp.full((req_count * capacity,), image_count, jnp.int32)
        .at[send_slot]
        .set(jnp.arange(image_count, dtype=jnp.int32))
    )
    outgoing = jnp.take(jnp.concatenate([image_cols, filler], axis=0), source_row, axis=0)
    incoming = lax.all_to_all(outgoing, "req", split_axis=0, concat_axis=0, tiled=True)
    arrival = (jnp.arange(req_count, dtype=jnp.int32)[:, None] * capacity + slot_index).reshape(-1)
    mine = (dest_group == req_index).astype(jnp.int32)
    rank = jnp.cumsum(mine) - mine
    total_images = image_dest.shape[0]
    pick = (
        jnp.zeros((image_count,), jnp.int32)
        .at[jnp.where(mine > 0, rank, image_count)]
        .set(jnp.arange(total_images, dtype=jnp.int32), mode="drop")
    )
    mine_cols = jnp.take(incoming, jnp.take(arrival, pick), axis=0)
    mine_rows = lax.all_to_all(
        jnp.broadcast_to(mine_cols[None], (blk_count,) + mine_cols.shape), BLK, 0, 0, tiled=False
    )
    mine_rows = mine_rows.transpose(1, 0, 2).reshape(image_count, -1)
    lookup = (
        jnp.full((tok_grp,), image_count, jnp.int32)
        .at[jnp.take(dest_local, pick)]
        .set(jnp.arange(image_count, dtype=jnp.int32))
    )
    choose = (lookup[:, None] == jnp.arange(image_count, dtype=jnp.int32)[None, :]).astype(
        jnp.bfloat16
    )
    placed = jnp.dot(choose, mine_rows, preferred_element_type=jnp.float32).astype(jnp.bfloat16)
    features = jnp.where((lookup < image_count)[:, None], placed, gathered_text)
    token_values = features.astype(jnp.float32)
    normed_tokens = (
        token_values
        * lax.rsqrt(jnp.mean(token_values * token_values, axis=-1, keepdims=True) + 1e-05)
        * text_gain.astype(jnp.float32)
    ).astype(jnp.bfloat16)
    positions, allowed = causal_setup(segment_ids[0])
    head_cols = query_weight.shape[1]
    qkv_weight = jnp.concatenate([query_weight, key_weight, value_weight], axis=1)
    qkv = jnp.dot(normed_tokens, qkv_weight, preferred_element_type=jnp.float32)
    queries = rotate(qkv[:, :head_cols], positions).astype(jnp.bfloat16)
    keys_rot = rotate(qkv[:, head_cols : 2 * head_cols], positions).astype(jnp.bfloat16)
    values_here = qkv[:, 2 * head_cols :].astype(jnp.bfloat16)
    block_rows = min(512, tok_grp)
    block_count = tok_grp // block_rows

    def attend_block(block_pair):
        return attend(block_pair[0], keys_rot, values_here, block_pair[1])

    attn_out = lax.map(
        attend_block,
        (
            queries.reshape(block_count, block_rows, -1),
            allowed.reshape(block_count, block_rows, tok_grp),
        ),
    ).reshape(tok_grp, -1)
    out_share = tok_grp // blk_count
    by_core = attn_out.reshape(blk_count // pair_count, pair_count, out_share, -1)
    from_quad = lax.all_to_all(by_core.transpose(1, 0, 2, 3), "quad", 0, 0, tiled=False)
    sources = (core_index - jnp.arange(pair_count, dtype=jnp.int32)) % pair_count
    in_order = jnp.take(from_quad, sources, axis=0)
    pair_attn = in_order.transpose(1, 2, 0, 3).reshape(tok_grp // pair_count, -1)
    pair_weight = jnp.concatenate(quad_weights, axis=0)
    pair_sum = jnp.dot(pair_attn, pair_weight, preferred_element_type=jnp.float32).astype(
        jnp.bfloat16
    )
    chip_count = blk_count // pair_count
    sums_here = lax.all_to_all(
        pair_sum.reshape(chip_count, out_share, -1), "grp", 0, 0, tiled=False
    )
    summed_heads = jnp.sum(sums_here.astype(jnp.float32), axis=0)
    residual = lax.dynamic_slice_in_dim(features, blk_index * out_share, out_share, 0).astype(
        jnp.float32
    )
    return (residual + summed_heads).astype(jnp.bfloat16)


BLK = ("grp", "quad")


def solution(mesh):
    blk_size, req_size = mesh.devices.shape
    pair_mesh = Mesh(mesh.devices.reshape(blk_size // 4, 4, req_size), ("grp", "quad", "req"))
    return jax.shard_map(
        body,
        mesh=pair_mesh,
        in_specs=(
            P("req", None),
            P(),
            P(),
            P(None, BLK),
            P(BLK),
            P(BLK, None),
            P(),
            P(),
            P(None, BLK),
            P(BLK),
            P(),
            P("req", BLK),
            P("req", None),
            P(),
            P(None, BLK),
            P(None, BLK),
            P(None, BLK),
            P(BLK, None),
        ),
        out_specs=P(("req",) + BLK, None),
        check_vma=False,
    )
```

```python
import jax
import jax.numpy as jnp
from jax import lax
from jax.sharding import Mesh, PartitionSpec as P

HEAD = 128


def layer_norm(values, gain_vector, shift_vector):
    centre = jnp.mean(values, axis=-1, keepdims=True)
    centred = values - centre
    spread = jnp.mean(centred * centred, axis=-1, keepdims=True)
    result = centred * lax.rsqrt(spread + 1e-06) * gain_vector.astype(jnp.float32)
    if shift_vector is None:
        return result
    return result + shift_vector.astype(jnp.float32)


def rotate(values, positions):
    half_size = HEAD // 2
    frequency = 10000.0 ** (-2.0 * jnp.arange(half_size, dtype=jnp.float32) / HEAD)
    angles = positions.astype(jnp.float32)[:, None] * frequency[None, :]
    cosine = jnp.cos(angles)[:, None, :]
    sine_table = jnp.sin(angles)[:, None, :]
    by_head = values.reshape(values.shape[0], -1, HEAD)
    first_half = by_head[..., :half_size]
    second_half = by_head[..., half_size:]
    turned = jnp.concatenate(
        [
            first_half * cosine - second_half * sine_table,
            second_half * cosine + first_half * sine_table,
        ],
        axis=-1,
    )
    return turned.reshape(values.shape)


def causal_setup(segments):
    length = segments.shape[0]
    column_ids = jnp.arange(length)
    same_request = segments[:, None] == segments[None, :]
    earlier = column_ids[None, :] < column_ids[:, None]
    positions = jnp.sum(same_request & earlier, axis=1)
    allowed = same_request & (column_ids[None, :] <= column_ids[:, None])
    return (positions, allowed)


def attend(queries, keys, values, allowed):
    row_count = queries.shape[0]
    key_count = keys.shape[0]
    query_heads = queries.reshape(row_count, -1, HEAD)
    key_heads = keys.reshape(key_count, -1, HEAD)
    value_heads = values.reshape(key_count, -1, HEAD)
    scores = jnp.einsum(
        "thd,shd->hts", query_heads, key_heads, preferred_element_type=jnp.float32
    ) * HEAD ** (-0.5)
    scores = jnp.where(allowed[None, :, :], scores, -jnp.inf)
    top_score = jnp.max(scores, axis=-1, keepdims=True)
    weights = jnp.exp(scores - top_score)
    weights = (weights / jnp.sum(weights, axis=-1, keepdims=True)).astype(jnp.bfloat16)
    mixed = jnp.einsum("hts,shd->thd", weights, value_heads, preferred_element_type=jnp.float32)
    return mixed.astype(jnp.bfloat16).reshape(row_count, -1)


def body(
    patches,
    vis_ln_gain,
    vis_ln_bias,
    vis_up,
    vis_up_bias,
    vis_down,
    vis_down_bias,
    merge_gain,
    merge_proj,
    merge_proj_bias,
    image_dest,
    text_embed,
    segment_ids,
    text_gain,
    query_weight,
    key_weight,
    value_weight,
    out_weight,
):
    pair_count = lax.axis_size("quad")
    blk_count = lax.axis_size("grp") * pair_count
    req_count = lax.axis_size("req")
    core_index = lax.axis_index("quad")
    blk_index = lax.axis_index("grp") * pair_count + core_index
    req_index = lax.axis_index("req")
    vis_width = patches.shape[1]
    gathered_text = lax.all_gather(text_embed, BLK, axis=1, tiled=True)
    quad_weights = [out_weight] + [
        lax.ppermute(
            out_weight, "quad", [(j, (j + shift) % pair_count) for j in range(pair_count)]
        )
        for shift in range(1, pair_count)
    ]
    patch_rows = patches.astype(jnp.float32)
    normed = layer_norm(patch_rows, vis_ln_gain, vis_ln_bias).astype(jnp.bfloat16)
    pre_act = jnp.dot(normed, vis_up, preferred_element_type=jnp.float32) + vis_up_bias.astype(
        jnp.float32
    )
    hidden = jax.nn.gelu(pre_act, approximate=False).astype(jnp.bfloat16)
    partial = jnp.dot(hidden, vis_down, preferred_element_type=jnp.float32).astype(jnp.bfloat16)
    patch_count = patches.shape[0]
    row_share = patch_count // blk_count
    parts_here = lax.all_to_all(
        partial.reshape(blk_count, row_share, vis_width), BLK, 0, 0, tiled=False
    )
    summed = jnp.sum(parts_here.astype(jnp.float32), axis=0)
    own_rows = lax.dynamic_slice_in_dim(patch_rows, blk_index * row_share, row_share, 0)
    vis_out = own_rows + summed + vis_down_bias.astype(jnp.float32)
    normed = layer_norm(vis_out, merge_gain, None).astype(jnp.bfloat16)
    merged_here = normed.reshape(-1, 4 * vis_width)
    merged_all = lax.all_to_all(
        jnp.broadcast_to(merged_here[None], (blk_count,) + merged_here.shape),
        BLK,
        0,
        0,
        tiled=False,
    )
    image_cols = jnp.dot(
        merged_all.reshape(-1, 4 * vis_width), merge_proj, preferred_element_type=jnp.float32
    )
    image_cols = (image_cols + merge_proj_bias.astype(jnp.float32)).astype(jnp.bfloat16)
    image_count = image_cols.shape[0]
    col_width = image_cols.shape[1]
    tok_grp = text_embed.shape[0]
    dest_group = image_dest // tok_grp
    dest_local = image_dest - dest_group * tok_grp
    target = jnp.where(dest_group == req_index, dest_local, tok_grp)
    filler = jnp.zeros((1, col_width), jnp.bfloat16)
    capacity = image_count // 4 + 3 * image_count // 4 // req_count
    by_source = dest_group.reshape(req_count, image_count)
    one_hot = (
        by_source[:, :, None] == jnp.arange(req_count, dtype=jnp.int32)[None, None, :]
    ).astype(jnp.int32)
    slot_index = jnp.sum((jnp.cumsum(one_hot, axis=1) - one_hot) * one_hot, axis=2)
    send_slot = lax.dynamic_index_in_dim(
        by_source * capacity + slot_index, req_index, 0, keepdims=False
    )
    source_row = (
        jnp.full((req_count * capacity,), image_count, jnp.int32)
        .at[send_slot]
        .set(jnp.arange(image_count, dtype=jnp.int32))
    )
    outgoing = jnp.take(jnp.concatenate([image_cols, filler], axis=0), source_row, axis=0)
    incoming = lax.all_to_all(outgoing, "req", split_axis=0, concat_axis=0, tiled=True)
    arrival = (jnp.arange(req_count, dtype=jnp.int32)[:, None] * capacity + slot_index).reshape(-1)
    mine = (dest_group == req_index).astype(jnp.int32)
    rank = jnp.cumsum(mine) - mine
    total_images = image_dest.shape[0]
    pick = (
        jnp.zeros((image_count,), jnp.int32)
        .at[jnp.where(mine > 0, rank, image_count)]
        .set(jnp.arange(total_images, dtype=jnp.int32), mode="drop")
    )
    mine_cols = jnp.take(incoming, jnp.take(arrival, pick), axis=0)
    mine_rows = lax.all_to_all(
        jnp.broadcast_to(mine_cols[None], (blk_count,) + mine_cols.shape), BLK, 0, 0, tiled=False
    )
    mine_rows = mine_rows.transpose(1, 0, 2).reshape(image_count, -1)
    lookup = (
        jnp.full((tok_grp,), image_count, jnp.int32)
        .at[jnp.take(dest_local, pick)]
        .set(jnp.arange(image_count, dtype=jnp.int32))
    )
    choose = (lookup[:, None] == jnp.arange(image_count, dtype=jnp.int32)[None, :]).astype(
        jnp.bfloat16
    )
    placed = jnp.dot(choose, mine_rows, preferred_element_type=jnp.float32).astype(jnp.bfloat16)
    features = jnp.where((lookup < image_count)[:, None], placed, gathered_text)
    token_values = features.astype(jnp.float32)
    normed_tokens = (
        token_values
        * lax.rsqrt(jnp.mean(token_values * token_values, axis=-1, keepdims=True) + 1e-05)
        * text_gain.astype(jnp.float32)
    ).astype(jnp.bfloat16)
    positions, allowed = causal_setup(segment_ids[0])
    head_cols = query_weight.shape[1]
    qkv_weight = jnp.concatenate([query_weight, key_weight, value_weight], axis=1)
    qkv = jnp.dot(normed_tokens, qkv_weight, preferred_element_type=jnp.float32)
    queries = rotate(qkv[:, :head_cols], positions).astype(jnp.bfloat16)
    keys_rot = rotate(qkv[:, head_cols : 2 * head_cols], positions).astype(jnp.bfloat16)
    values_here = qkv[:, 2 * head_cols :].astype(jnp.bfloat16)
    block_rows = tok_grp
    block_count = tok_grp // block_rows

    def attend_block(block_pair):
        return attend(block_pair[0], keys_rot, values_here, block_pair[1])

    attn_out = lax.map(
        attend_block,
        (
            queries.reshape(block_count, block_rows, -1),
            allowed.reshape(block_count, block_rows, tok_grp),
        ),
    ).reshape(tok_grp, -1)
    out_share = tok_grp // blk_count
    by_core = attn_out.reshape(blk_count // pair_count, pair_count, out_share, -1)
    from_quad = lax.all_to_all(by_core.transpose(1, 0, 2, 3), "quad", 0, 0, tiled=False)
    sources = (core_index - jnp.arange(pair_count, dtype=jnp.int32)) % pair_count
    in_order = jnp.take(from_quad, sources, axis=0)
    pair_attn = in_order.transpose(1, 2, 0, 3).reshape(tok_grp // pair_count, -1)
    pair_weight = jnp.concatenate(quad_weights, axis=0)
    pair_sum = jnp.dot(pair_attn, pair_weight, preferred_element_type=jnp.float32).astype(
        jnp.bfloat16
    )
    chip_count = blk_count // pair_count
    sums_here = lax.all_to_all(
        pair_sum.reshape(chip_count, out_share, -1), "grp", 0, 0, tiled=False
    )
    summed_heads = jnp.sum(sums_here.astype(jnp.float32), axis=0)
    residual = lax.dynamic_slice_in_dim(features, blk_index * out_share, out_share, 0).astype(
        jnp.float32
    )
    return (residual + summed_heads).astype(jnp.bfloat16)


BLK = ("grp", "quad")


def solution(mesh):
    blk_size, req_size = mesh.devices.shape
    pair_mesh = Mesh(mesh.devices.reshape(blk_size // 4, 4, req_size), ("grp", "quad", "req"))
    return jax.shard_map(
        body,
        mesh=pair_mesh,
        in_specs=(
            P("req", None),
            P(),
            P(),
            P(None, BLK),
            P(BLK),
            P(BLK, None),
            P(),
            P(),
            P(None, BLK),
            P(BLK),
            P(),
            P("req", BLK),
            P("req", None),
            P(),
            P(None, BLK),
            P(None, BLK),
            P(None, BLK),
            P(BLK, None),
        ),
        out_specs=P(("req",) + BLK, None),
        check_vma=False,
    )
```
